32 devices in a mesh: groups: 2 (over y), row: 4 (over x, core), col: 4 (over z).
Axes of the slice: x: 2, y: 2, z: 4, core: 2. Of those that a mesh axis runs over, the one named last changes fastest.
Arguments:
- tokens: float32 [256, 8192], P(('groups', 'row', 'col')), parts along dimension 0, may hold values from -36 to 36
- modulation: float32 [3, 2, 8192], P(None, 'groups'), parts along dimension 1, may hold values from -4 to 4
- up_weight: float32 [8192, 16384], P('row', 'col'), may hold values from -0.0625 to 0.0625
- up_bias: float32 [16384], P('col'), may hold values from -3 to 3
- down_weight: float32 [16384, 8192], P('col', 'row'), may hold values from -0.046875 to 0.046875
- down_bias: float32 [8192], replicated, may hold values from -3 to 3
Outputs:
- result: float32 [256, 8192], P(('groups', 'row', 'col')), parts along dimension 0
The draws below stay inside these ranges and needn't reach their ends.
There are 2 independent parts, one for each index of `groups`. The reference program is written for one: setup_inputs(seed, part) draws one part's arguments, and reference() takes and returns one part's arrays. A program takes and returns all parts, laid end to end along the dimension named above; an argument that names none is the same for every part. Nothing has to cross between parts.
All inputs are finite; a program needn't handle non-finite values.
Results may differ from the reference program's by a relative error of at most 0.00005.
Values sent between devices are 32-bit elements; how exact they have to be, the bound alone decides.
No kernel may reach another device: no remote copies, remote signals or barrier semaphores. Data moves between devices by JAX's collectives and lax.ppermute only.
A program may use at most 128 MiB of HBM per device.

```python
import math
import jax
import jax.numpy as jnp
from jax import lax

D = 8192
FF = 16384
SEQ = 256
TOKENS = 128
SAMPLES = 1


def draw_tokens(key, part):
    key_base = jax.random.fold_in(key, 11)
    key_rows = jax.random.fold_in(key, 12)
    key_cols = jax.random.fold_in(key, 13)
    row_scale = jnp.exp(jax.random.uniform(key_rows, (TOKENS, 1), jnp.float32, math.log(0.3), math.log(3.0)))
    col_scale = jnp.exp(jax.random.uniform(key_cols, (1, D), jnp.float32, math.log(0.3), math.log(3.0)))
    base_vals = jnp.clip(jax.random.normal(key_base, (TOKENS, D), jnp.float32), -4.0, 4.0)
    return base_vals * row_scale * col_scale


def level_of(own_key, dims, split, low, top_value):
    factor_of, own = 1.0, jax.random.fold_in(own_key, 6)
    for dim, parts in split:
        heights = jnp.exp(jax.random.uniform(jax.random.fold_in(own, dim), (parts,), jnp.float32, low / len(split), top_value / len(split)))
        factor_of = factor_of * jnp.repeat(heights, dims[dim] // parts).reshape([-1 if axis == dim else 1 for axis in range(len(dims))])
    return factor_of


def bell_draw(own_key, dims, width, bound, shards=(), held_as=jnp.bfloat16):
    values = width * jax.random.normal(own_key, dims, jnp.float32)
    if shards:
        values = values * level_of(own_key, dims, shards, -0.22, 0.18)
    return jnp.clip(values, -bound, bound).astype(held_as)


def setup_inputs(seed: int = 0, part: int = 0) -> dict:
    streams_of = jax.random.split(jax.random.key(seed), 7)
    own_keys = jax.random.split(jax.random.fold_in(streams_of[6], part), 7)
    return {
        "tokens": draw_tokens(jax.random.fold_in(jax.random.fold_in(streams_of[6], part), 71), part),
        "modulation": bell_draw(own_keys[1], (3, SAMPLES, D), 0.7, 4.0, (), jnp.float32),
        "up_weight": bell_draw(streams_of[2], (D, FF), D ** -0.5, 0.0625, ((0, 4), (1, 4)), jnp.float32),
        "up_bias": bell_draw(streams_of[3], (FF,), 0.5, 3.0, ((0, 4),), jnp.float32),
        "down_weight": bell_draw(streams_of[4], (FF, D), FF ** -0.5, 0.046875, ((0, 4), (1, 4)), jnp.float32),
        "down_bias": bell_draw(streams_of[5], (D,), 0.5, 3.0, (), jnp.float32),
    }


layer_eps = 1e-06

def reference(tokens, modulation, up_weight, up_bias, down_weight, down_bias):
    sample_ids = jnp.arange(TOKENS, dtype=jnp.int32) // SEQ
    shift_tok = modulation[0][sample_ids]
    scale_tok = modulation[1][sample_ids]
    gate_tok = modulation[2][sample_ids]
    average = lax.optimization_barrier(jnp.mean(tokens, axis=1, keepdims=True))
    centred = tokens - average
    spread_sq = lax.optimization_barrier(jnp.mean(centred * centred, axis=1, keepdims=True))
    normed = centred * lax.rsqrt(spread_sq + layer_eps)
    mixed = normed * (1.0 + scale_tok) + shift_tok
    hidden = jnp.dot(mixed, up_weight, precision=lax.Precision.HIGHEST, preferred_element_type=jnp.float32) + up_bias
    activated = jax.nn.gelu(hidden, approximate=True)
    branch = jnp.dot(activated, down_weight, precision=lax.Precision.HIGHEST, preferred_element_type=jnp.float32) + down_bias
    return tokens + gate_tok * branch
```

```python
import jax
import jax.numpy as jnp
from jax import lax
from jax.sharding import PartitionSpec as P

SEQ = 256


layer_eps = 1e-06


def local(tokens, modulation, up_weight, up_bias, down_weight, down_bias):
    tok_dev = tokens.shape[0]
    first_tok = (lax.axis_index("row") * lax.axis_size("col") + lax.axis_index("col")) * tok_dev
    sample = first_tok // SEQ
    own_mods = lax.dynamic_slice_in_dim(modulation, sample, 1, 1)[:, 0]
    shift_vec = own_mods[0]
    scale_vec = own_mods[1]
    gate_vec = own_mods[2]
    average = jnp.mean(tokens, axis=1, keepdims=True)
    centred = tokens - average
    spread_sq = jnp.mean(centred * centred, axis=1, keepdims=True)
    normed = centred * lax.rsqrt(spread_sq + layer_eps)
    mixed = normed * (1.0 + scale_vec) + shift_vec
    columns = lax.all_to_all(mixed, "row", split_axis=1, concat_axis=0, tiled=True)
    partial_value = jnp.dot(
        lax.all_gather(columns, "col", axis=0, tiled=True),
        up_weight,
        precision=lax.Precision.HIGH,
        preferred_element_type=jnp.float32,
    )
    own_share = lax.psum_scatter(partial_value, "row", scatter_dimension=0, tiled=True)
    activated_share = jax.nn.gelu(own_share + up_bias, approximate=True)
    activated = lax.all_gather(activated_share, "row", axis=0, tiled=True)
    out_share = lax.psum_scatter(
        jnp.dot(
            activated,
            down_weight,
            precision=lax.Precision.HIGH,
            preferred_element_type=jnp.float32,
        ),
        "col",
        scatter_dimension=0,
        tiled=True,
    )
    returned = lax.all_to_all(out_share, "row", split_axis=0, concat_axis=1, tiled=True)
    return tokens + gate_vec * (returned + down_bias)


def solution(mesh):
    in_specs = (
        P(("groups", "row", "col"), None),
        P(None, "groups", None),
        P("row", "col"),
        P("col"),
        P("col", "row"),
        P(),
    )
    out_specs = P(("groups", "row", "col"), None)
    return jax.shard_map(local, mesh=mesh, in_specs=in_specs, out_specs=out_specs, check_vma=False)
```

```python
import jax
import jax.numpy as jnp
from jax import lax
from jax.sharding import PartitionSpec as P

SEQ = 256


layer_eps = 1e-06


def _pairs(n, flip):
    return [(i, i ^ flip) for i in range(n)]


def local(tokens, modulation, up_weight, up_bias, down_weight, down_bias):
    n_row = lax.axis_size("row")
    tok_dev = tokens.shape[0]
    first_tok = (lax.axis_index("row") * lax.axis_size("col") + lax.axis_index("col")) * tok_dev
    sample = first_tok // SEQ
    own_mods = lax.dynamic_slice_in_dim(modulation, sample, 1, 1)[:, 0]
    shift_vec = own_mods[0]
    scale_vec = own_mods[1]
    gate_vec = own_mods[2]
    average = jnp.mean(tokens, axis=1, keepdims=True)
    centred = tokens - average
    spread_sq = jnp.mean(centred * centred, axis=1, keepdims=True)
    normed = centred * lax.rsqrt(spread_sq + layer_eps)
    mixed = normed * (1.0 + scale_vec) + shift_vec
    columns = lax.all_to_all(mixed, "row", split_axis=1, concat_axis=0, tiled=True)
    gathered = lax.all_gather(columns, "col", axis=0, tiled=True)
    hidden = jnp.dot(gathered, up_weight, precision=lax.Precision.HIGH,
                     preferred_element_type=jnp.float32)
    n_pos, ff_blk = hidden.shape
    quarter = ff_blk // n_row
    r = lax.axis_index("row")
    buf = hidden.reshape(n_pos, n_row, quarter)
    flip = 1
    while flip < n_row:
        bit = (r // flip) % 2
        pairs = buf.reshape(n_pos, buf.shape[1] // 2, 2, quarter)
        keep = jnp.where(bit == 0, pairs[:, :, 0], pairs[:, :, 1])
        send = jnp.where(bit == 0, pairs[:, :, 1], pairs[:, :, 0])
        buf = keep + lax.ppermute(send, "row", _pairs(n_row, flip))
        flip *= 2
    bias_q = lax.dynamic_slice_in_dim(up_bias, r * quarter, quarter)
    act = jax.nn.gelu(buf + bias_q[None, None, :], approximate=True)
    flip = n_row // 2
    while flip >= 1:
        bit = (r // flip) % 2
        other = lax.ppermute(act, "row", _pairs(n_row, flip))
        act = jnp.where(bit == 0, jnp.stack([act, other], axis=2), jnp.stack([other, act], axis=2))
        act = act.reshape(n_pos, act.shape[1] * 2, quarter)
        flip //= 2
    act = act.reshape(n_pos, ff_blk)
    partial_out = jnp.dot(act, down_weight, precision=lax.Precision.HIGH,
                          preferred_element_type=jnp.float32)
    out_share = lax.psum_scatter(partial_out, "col", scatter_dimension=0, tiled=True)
    returned = lax.all_to_all(out_share, "row", split_axis=0, concat_axis=1, tiled=True)
    return tokens + gate_vec * (returned + down_bias)


def solution(mesh):
    in_specs = (
        P(("groups", "row", "col"), None),
        P(None, "groups", None),
        P("row", "col"),
        P("col"),
        P("col", "row"),
        P(),
    )
    out_specs = P(("groups", "row", "col"), None)
    return jax.shard_map(local, mesh=mesh, in_specs=in_specs, out_specs=out_specs, check_vma=False)
```

```python
import jax
import jax.numpy as jnp
from jax import lax
from jax.sharding import PartitionSpec as P

SEQ = 256


layer_eps = 1e-06


def _pairs(n, flip):
    return [(i, i ^ flip) for i in range(n)]


def local(tokens, modulation, up_weight, up_bias, down_weight, down_bias):
    n_row = lax.axis_size("row")
    tok_dev = tokens.shape[0]
    first_tok = (lax.axis_index("row") * lax.axis_size("col") + lax.axis_index("col")) * tok_dev
    sample = first_tok // SEQ
    own_mods = lax.dynamic_slice_in_dim(modulation, sample, 1, 1)[:, 0]
    shift_vec = own_mods[0]
    scale_vec = own_mods[1]
    gate_vec = own_mods[2]
    average = jnp.mean(tokens, axis=1, keepdims=True)
    centred = tokens - average
    spread_sq = jnp.mean(centred * centred, axis=1, keepdims=True)
    normed = centred * lax.rsqrt(spread_sq + layer_eps)
    mixed = normed * (1.0 + scale_vec) + shift_vec
    columns = lax.all_to_all(mixed, "row", split_axis=1, concat_axis=0, tiled=True)
    gathered = lax.all_gather(columns, "col", axis=0, tiled=True)
    n_pos = gathered.shape[0]
    ff_blk = up_weight.shape[1]
    quarter = ff_blk // n_row
    r = lax.axis_index("row")

    def up_block(d):
        w = lax.dynamic_slice_in_dim(up_weight, (r ^ d) * quarter, quarter, 1)
        return jnp.dot(gathered, w, precision=lax.Precision.HIGH,
                       preferred_element_type=jnp.float32)

    held = {d: lax.optimization_barrier(up_block(d)) for d in range(n_row)}
    flip = 1
    while flip < n_row:
        sent = [d for d in sorted(held) if d & flip]
        got = lax.ppermute(jnp.stack([held[d] for d in sent]), "row", _pairs(n_row, flip))
        held = {d ^ flip: held[d ^ flip] + got[i] for i, d in enumerate(sent)}
        flip *= 2
    bias_q = lax.dynamic_slice_in_dim(up_bias, r * quarter, quarter)
    acts = {0: jax.nn.gelu(held[0] + bias_q[None, :], approximate=True)}
    acts[1] = lax.ppermute(acts[0], "row", _pairs(n_row, 1))
    flip = 2
    while flip < n_row:
        mine = sorted(d for d in acts if d % 2 == 0)
        got = lax.ppermute(jnp.stack([acts[d] for d in mine]), "row", _pairs(n_row, flip))
        for i, d in enumerate(mine):
            acts[d ^ flip] = got[i]
        flip *= 2
    def down_term(d):
        w = lax.dynamic_slice_in_dim(down_weight, (r ^ d) * quarter, quarter, 0)
        return jnp.dot(acts[d], w, precision=lax.Precision.HIGH,
                       preferred_element_type=jnp.float32)

    partial_out = down_term(0) + down_term(1)
    far = sorted(d for d in acts if d % 2 == 0 and d != 0)
    if far:
        stacked, partial_out = lax.optimization_barrier(
            (jnp.stack([acts[d] for d in far]), partial_out))
        got = lax.ppermute(stacked, "row", _pairs(n_row, 1))
        for i, d in enumerate(far):
            acts[d ^ 1] = got[i]
        for d in far:
            partial_out = partial_out + down_term(d)
        for d in far:
            partial_out = partial_out + down_term(d ^ 1)
    out_share = lax.psum_scatter(partial_out, "col", scatter_dimension=0, tiled=True)
    returned = lax.all_to_all(out_share, "row", split_axis=0, concat_axis=1, tiled=True)
    return tokens + gate_vec * (returned + down_bias)


def solution(mesh):
    in_specs = (
        P(("groups", "row", "col"), None),
        P(None, "groups", None),
        P("row", "col"),
        P("col"),
        P("col", "row"),
        P(),
    )
    out_specs = P(("groups", "row", "col"), None)
    return jax.shard_map(local, mesh=mesh, in_specs=in_specs, out_specs=out_specs, check_vma=False)
```

```python
import jax
import jax.numpy as jnp
from jax import lax
from jax.sharding import PartitionSpec as P

SEQ = 256


layer_eps = 1e-06


def _pairs(n, flip):
    return [(i, i ^ flip) for i in range(n)]


def _gather_rel(x, axis, n):
    held = {0: x}
    flip = n // 2
    while flip >= 1:
        keys = sorted(held)
        got = lax.ppermute(jnp.stack([held[k] for k in keys]), axis, _pairs(n, flip))
        for i, k in enumerate(keys):
            held[k ^ flip] = got[i]
        flip //= 2
    return jnp.concatenate([held[d] for d in range(n)], axis=0)


def _scatter_rel(x, axis, n):
    blk = x.shape[0] // n
    held = {d: x[d * blk:(d + 1) * blk] for d in range(n)}
    flip = 1
    while flip < n:
        sent = [d for d in sorted(held) if d & flip]
        got = lax.ppermute(jnp.stack([held[d] for d in sent]), axis, _pairs(n, flip))
        held = {d ^ flip: held[d ^ flip] + got[i] for i, d in enumerate(sent)}
        flip *= 2
    return held[0]


def local(tokens, modulation, up_weight, up_bias, down_weight, down_bias):
    n_row = lax.axis_size("row")
    tok_dev = tokens.shape[0]
    first_tok = (lax.axis_index("row") * lax.axis_size("col") + lax.axis_index("col")) * tok_dev
    sample = first_tok // SEQ
    own_mods = lax.dynamic_slice_in_dim(modulation, sample, 1, 1)[:, 0]
    shift_vec = own_mods[0]
    scale_vec = own_mods[1]
    gate_vec = own_mods[2]
    average = jnp.mean(tokens, axis=1, keepdims=True)
    centred = tokens - average
    spread_sq = jnp.mean(centred * centred, axis=1, keepdims=True)
    normed = centred * lax.rsqrt(spread_sq + layer_eps)
    mixed = normed * (1.0 + scale_vec) + shift_vec
    columns = lax.all_to_all(mixed, "row", split_axis=1, concat_axis=0, tiled=True)
    n_col = lax.axis_size("col")
    gathered = _gather_rel(columns, "col", n_col)
    n_pos = gathered.shape[0]
    ff_blk = up_weight.shape[1]
    quarter = ff_blk // n_row
    r = lax.axis_index("row")

    def up_block(d):
        w = lax.dynamic_slice_in_dim(up_weight, (r ^ d) * quarter, quarter, 1)
        return jnp.dot(gathered, w, precision=lax.Precision.HIGH,
                       preferred_element_type=jnp.float32)

    held = {d: lax.optimization_barrier(up_block(d)) for d in range(n_row)}
    flip = 1
    while flip < n_row:
        sent = [d for d in sorted(held) if d & flip]
        got = lax.ppermute(jnp.stack([held[d] for d in sent]), "row", _pairs(n_row, flip))
        held = {d ^ flip: held[d ^ flip] + got[i] for i, d in enumerate(sent)}
        flip *= 2
    bias_q = lax.dynamic_slice_in_dim(up_bias, r * quarter, quarter)
    acts = {0: jax.nn.gelu(held[0] + bias_q[None, :], approximate=True)}
    acts[1] = lax.ppermute(acts[0], "row", _pairs(n_row, 1))
    flip = 2
    while flip < n_row:
        mine = sorted(d for d in acts if d % 2 == 0)
        got = lax.ppermute(jnp.stack([acts[d] for d in mine]), "row", _pairs(n_row, flip))
        for i, d in enumerate(mine):
            acts[d ^ flip] = got[i]
        flip *= 2
    def down_term(d):
        w = lax.dynamic_slice_in_dim(down_weight, (r ^ d) * quarter, quarter, 0)
        return jnp.dot(acts[d], w, precision=lax.Precision.HIGH,
                       preferred_element_type=jnp.float32)

    partial_out = down_term(0) + down_term(1)
    far = sorted(d for d in acts if d % 2 == 0 and d != 0)
    if far:
        stacked, partial_out = lax.optimization_barrier(
            (jnp.stack([acts[d] for d in far]), partial_out))
        got = lax.ppermute(stacked, "row", _pairs(n_row, 1))
        for i, d in enumerate(far):
            acts[d ^ 1] = got[i]
        for d in far:
            partial_out = partial_out + down_term(d)
        for d in far:
            partial_out = partial_out + down_term(d ^ 1)
    out_share = _scatter_rel(partial_out, "col", n_col)
    returned = lax.all_to_all(out_share, "row", split_axis=0, concat_axis=1, tiled=True)
    return tokens + gate_vec * (returned + down_bias)


def solution(mesh):
    in_specs = (
        P(("groups", "row", "col"), None),
        P(None, "groups", None),
        P("row", "col"),
        P("col"),
        P("col", "row"),
        P(),
    )
    out_specs = P(("groups", "row", "col"), None)
    return jax.shard_map(local, mesh=mesh, in_specs=in_specs, out_specs=out_specs, check_vma=False)
```

```python
import jax
import jax.numpy as jnp
from jax import lax
from jax.sharding import PartitionSpec as P

SEQ = 256


layer_eps = 1e-06


def _pairs(n, flip):
    return [(i, i ^ flip) for i in range(n)]


def _gather_rel(x, axis, n):
    held = {0: x}
    flip = n // 2
    while flip >= 1:
        keys = sorted(held)
        got = lax.ppermute(jnp.stack([held[k] for k in keys]), axis, _pairs(n, flip))
        for i, k in enumerate(keys):
            held[k ^ flip] = got[i]
        flip //= 2
    return jnp.concatenate([held[d] for d in range(n)], axis=0)


def _scatter_rel(x, axis, n):
    blk = x.shape[0] // n
    held = {d: x[d * blk:(d + 1) * blk] for d in range(n)}
    flip = 1
    while flip < n:
        sent = [d for d in sorted(held) if d & flip]
        got = lax.ppermute(jnp.stack([held[d] for d in sent]), axis, _pairs(n, flip))
        held = {d ^ flip: held[d ^ flip] + got[i] for i, d in enumerate(sent)}
        flip *= 2
    return held[0]


def _exchange_abs(blocks, axis, n, idx):
    got = [blocks[idx]]
    for d in range(1, n):
        got.append(lax.ppermute(blocks[idx ^ d], axis, _pairs(n, d)))
    rel = jnp.stack(got)
    return jnp.stack([rel[s ^ idx] for s in range(n)])


def local(tokens, modulation, up_weight, up_bias, down_weight, down_bias):
    n_row = lax.axis_size("row")
    tok_dev = tokens.shape[0]
    first_tok = (lax.axis_index("row") * lax.axis_size("col") + lax.axis_index("col")) * tok_dev
    sample = first_tok // SEQ
    own_mods = lax.dynamic_slice_in_dim(modulation, sample, 1, 1)[:, 0]
    shift_vec = own_mods[0]
    scale_vec = own_mods[1]
    gate_vec = own_mods[2]
    average = jnp.mean(tokens, axis=1, keepdims=True)
    centred = tokens - average
    spread_sq = jnp.mean(centred * centred, axis=1, keepdims=True)
    normed = centred * lax.rsqrt(spread_sq + layer_eps)
    mixed = normed * (1.0 + scale_vec) + shift_vec
    r = lax.axis_index("row")
    d_blk = mixed.shape[1] // n_row
    sent_in = mixed.reshape(tok_dev, n_row, d_blk).swapaxes(0, 1)
    columns = _exchange_abs(sent_in, "row", n_row, r).reshape(n_row * tok_dev, d_blk)
    n_col = lax.axis_size("col")
    gathered = _gather_rel(columns, "col", n_col)
    n_pos = gathered.shape[0]
    ff_blk = up_weight.shape[1]
    quarter = ff_blk // n_row

    def up_block(d):
        w = lax.dynamic_slice_in_dim(up_weight, (r ^ d) * quarter, quarter, 1)
        return jnp.dot(gathered, w, precision=lax.Precision.HIGH,
                       preferred_element_type=jnp.float32)

    held = {d: lax.optimization_barrier(up_block(d)) for d in range(n_row)}
    flip = 1
    while flip < n_row:
        sent = [d for d in sorted(held) if d & flip]
        got = lax.ppermute(jnp.stack([held[d] for d in sent]), "row", _pairs(n_row, flip))
        held = {d ^ flip: held[d ^ flip] + got[i] for i, d in enumerate(sent)}
        flip *= 2
    bias_q = lax.dynamic_slice_in_dim(up_bias, r * quarter, quarter)
    acts = {0: jax.nn.gelu(held[0] + bias_q[None, :], approximate=True)}
    acts[1] = lax.ppermute(acts[0], "row", _pairs(n_row, 1))
    flip = 2
    while flip < n_row:
        mine = sorted(d for d in acts if d % 2 == 0)
        got = lax.ppermute(jnp.stack([acts[d] for d in mine]), "row", _pairs(n_row, flip))
        for i, d in enumerate(mine):
            acts[d ^ flip] = got[i]
        flip *= 2
    def down_term(d):
        w = lax.dynamic_slice_in_dim(down_weight, (r ^ d) * quarter, quarter, 0)
        return jnp.dot(acts[d], w, precision=lax.Precision.HIGH,
                       preferred_element_type=jnp.float32)

    partial_out = down_term(0) + down_term(1)
    far = sorted(d for d in acts if d % 2 == 0 and d != 0)
    if far:
        stacked, partial_out = lax.optimization_barrier(
            (jnp.stack([acts[d] for d in far]), partial_out))
        got = lax.ppermute(stacked, "row", _pairs(n_row, 1))
        for i, d in enumerate(far):
            acts[d ^ 1] = got[i]
        for d in far:
            partial_out = partial_out + down_term(d)
        for d in far:
            partial_out = partial_out + down_term(d ^ 1)
    out_share = _scatter_rel(partial_out, "col", n_col)
    back = _exchange_abs(out_share.reshape(n_row, tok_dev, d_blk), "row", n_row, r)
    returned = back.swapaxes(0, 1).reshape(tok_dev, n_row * d_blk)
    return tokens + gate_vec * (returned + down_bias)


def solution(mesh):
    in_specs = (
        P(("groups", "row", "col"), None),
        P(None, "groups", None),
        P("row", "col"),
        P("col"),
        P("col", "row"),
        P(),
    )
    out_specs = P(("groups", "row", "col"), None)
    return jax.shard_map(local, mesh=mesh, in_specs=in_specs, out_specs=out_specs, check_vma=False)
```

```python
import jax
import jax.numpy as jnp
from jax import lax
from jax.sharding import PartitionSpec as P

SEQ = 256
N_CHUNK = 2


layer_eps = 1e-06


def _pairs(n, flip):
    return [(i, i ^ flip) for i in range(n)]


def _gather_rel(x, axis, n):
    held = {0: x}
    flip = n // 2
    while flip >= 1:
        keys = sorted(held)
        got = lax.ppermute(jnp.stack([held[k] for k in keys]), axis, _pairs(n, flip))
        for i, k in enumerate(keys):
            held[k ^ flip] = got[i]
        flip //= 2
    return jnp.concatenate([held[d] for d in range(n)], axis=0)


def _scatter_rel(x, axis, n):
    blk = x.shape[0] // n
    held = {d: x[d * blk:(d + 1) * blk] for d in range(n)}
    flip = 1
    while flip < n:
        sent = [d for d in sorted(held) if d & flip]
        got = lax.ppermute(jnp.stack([held[d] for d in sent]), axis, _pairs(n, flip))
        held = {d ^ flip: held[d ^ flip] + got[i] for i, d in enumerate(sent)}
        flip *= 2
    return held[0]


def _exchange_abs(blocks, axis, n, idx):
    got = [blocks[idx]]
    for d in range(1, n):
        got.append(lax.ppermute(blocks[idx ^ d], axis, _pairs(n, d)))
    rel = jnp.stack(got)
    return jnp.stack([rel[s ^ idx] for s in range(n)])


def local(tokens, modulation, up_weight, up_bias, down_weight, down_bias):
    n_row = lax.axis_size("row")
    tok_dev = tokens.shape[0]
    first_tok = (lax.axis_index("row") * lax.axis_size("col") + lax.axis_index("col")) * tok_dev
    sample = first_tok // SEQ
    own_mods = lax.dynamic_slice_in_dim(modulation, sample, 1, 1)[:, 0]
    shift_vec = own_mods[0]
    scale_vec = own_mods[1]
    gate_vec = own_mods[2]
    average = jnp.mean(tokens, axis=1, keepdims=True)
    centred = tokens - average
    spread_sq = jnp.mean(centred * centred, axis=1, keepdims=True)
    normed = centred * lax.rsqrt(spread_sq + layer_eps)
    mixed = normed * (1.0 + scale_vec) + shift_vec
    r = lax.axis_index("row")
    d_blk = mixed.shape[1] // n_row
    sent_in = mixed.reshape(tok_dev, n_row, d_blk).swapaxes(0, 1)
    columns = _exchange_abs(sent_in, "row", n_row, r).reshape(n_row * tok_dev, d_blk)
    n_col = lax.axis_size("col")
    chunk = columns.shape[0] // N_CHUNK
    gathered = jnp.concatenate(
        [_gather_rel(columns[i * chunk:(i + 1) * chunk], "col", n_col) for i in range(N_CHUNK)],
        axis=0)
    n_pos = gathered.shape[0]
    ff_blk = up_weight.shape[1]
    quarter = ff_blk // n_row

    def up_block(d):
        w = lax.dynamic_slice_in_dim(up_weight, (r ^ d) * quarter, quarter, 1)
        return jnp.dot(gathered, w, precision=lax.Precision.HIGH,
                       preferred_element_type=jnp.float32)

    held = {d: lax.optimization_barrier(up_block(d)) for d in range(n_row)}
    flip = 1
    while flip < n_row:
        sent = [d for d in sorted(held) if d & flip]
        got = lax.ppermute(jnp.stack([held[d] for d in sent]), "row", _pairs(n_row, flip))
        held = {d ^ flip: held[d ^ flip] + got[i] for i, d in enumerate(sent)}
        flip *= 2
    bias_q = lax.dynamic_slice_in_dim(up_bias, r * quarter, quarter)
    acts = {0: jax.nn.gelu(held[0] + bias_q[None, :], approximate=True)}
    acts[1] = lax.ppermute(acts[0], "row", _pairs(n_row, 1))
    flip = 2
    while flip < n_row:
        mine = sorted(d for d in acts if d % 2 == 0)
        got = lax.ppermute(jnp.stack([acts[d] for d in mine]), "row", _pairs(n_row, flip))
        for i, d in enumerate(mine):
            acts[d ^ flip] = got[i]
        flip *= 2
    def down_term(d):
        w = lax.dynamic_slice_in_dim(down_weight, (r ^ d) * quarter, quarter, 0)
        return jnp.dot(acts[d], w, precision=lax.Precision.HIGH,
                       preferred_element_type=jnp.float32)

    partial_out = down_term(0) + down_term(1)
    far = sorted(d for d in acts if d % 2 == 0 and d != 0)
    if far:
        stacked, partial_out = lax.optimization_barrier(
            (jnp.stack([acts[d] for d in far]), partial_out))
        got = lax.ppermute(stacked, "row", _pairs(n_row, 1))
        for i, d in enumerate(far):
            acts[d ^ 1] = got[i]
        for d in far:
            partial_out = partial_out + down_term(d)
        for d in far:
            partial_out = partial_out + down_term(d ^ 1)
    per_chunk = partial_out.shape[0] // N_CHUNK
    out_share = jnp.concatenate(
        [_scatter_rel(partial_out[i * per_chunk:(i + 1) * per_chunk], "col", n_col)
         for i in range(N_CHUNK)], axis=0)
    back = _exchange_abs(out_share.reshape(n_row, tok_dev, d_blk), "row", n_row, r)
    returned = back.swapaxes(0, 1).reshape(tok_dev, n_row * d_blk)
    return tokens + gate_vec * (returned + down_bias)


def solution(mesh):
    in_specs = (
        P(("groups", "row", "col"), None),
        P(None, "groups", None),
        P("row", "col"),
        P("col"),
        P("col", "row"),
        P(),
    )
    out_specs = P(("groups", "row", "col"), None)
    return jax.shard_map(local, mesh=mesh, in_specs=in_specs, out_specs=out_specs, check_vma=False)
```

```python
import jax
import jax.numpy as jnp
from jax import lax
from jax.sharding import PartitionSpec as P

SEQ = 256
N_CHUNK = 2


layer_eps = 1e-06


def _pairs(n, flip):
    return [(i, i ^ flip) for i in range(n)]


def _gather_rel(x, axis, n):
    held = {0: x}
    flip = n // 2
    while flip >= 1:
        keys = sorted(held)
        got = lax.ppermute(jnp.stack([held[k] for k in keys]), axis, _pairs(n, flip))
        for i, k in enumerate(keys):
            held[k ^ flip] = got[i]
        flip //= 2
    return jnp.concatenate([held[d] for d in range(n)], axis=0)


def _scatter_rel(x, axis, n):
    blk = x.shape[0] // n
    held = {d: x[d * blk:(d + 1) * blk] for d in range(n)}
    flip = 1
    while flip < n:
        sent = [d for d in sorted(held) if d & flip]
        got = lax.ppermute(jnp.stack([held[d] for d in sent]), axis, _pairs(n, flip))
        held = {d ^ flip: held[d ^ flip] + got[i] for i, d in enumerate(sent)}
        flip *= 2
    return held[0]


def _exchange_abs(blocks, axis, n, idx):
    got = [blocks[idx]]
    for d in range(1, n):
        got.append(lax.ppermute(blocks[idx ^ d], axis, _pairs(n, d)))
    rel = jnp.stack(got)
    return jnp.stack([rel[s ^ idx] for s in range(n)])


def local(tokens, modulation, up_weight, up_bias, down_weight, down_bias):
    n_row = lax.axis_size("row")
    tok_dev = tokens.shape[0]
    first_tok = (lax.axis_index("row") * lax.axis_size("col") + lax.axis_index("col")) * tok_dev
    sample = first_tok // SEQ
    own_mods = lax.dynamic_slice_in_dim(modulation, sample, 1, 1)[:, 0]
    shift_vec = own_mods[0]
    scale_vec = own_mods[1]
    gate_vec = own_mods[2]
    average = jnp.mean(tokens, axis=1, keepdims=True)
    centred = tokens - average
    spread_sq = jnp.mean(centred * centred, axis=1, keepdims=True)
    normed = centred * lax.rsqrt(spread_sq + layer_eps)
    mixed = normed * (1.0 + scale_vec) + shift_vec
    r = lax.axis_index("row")
    d_blk = mixed.shape[1] // n_row
    sent_in = mixed.reshape(tok_dev, n_row, d_blk).swapaxes(0, 1)
    columns = _exchange_abs(sent_in, "row", n_row, r).reshape(n_row * tok_dev, d_blk)
    n_col = lax.axis_size("col")
    chunk = columns.shape[0] // N_CHUNK
    gathered = jnp.concatenate(
        [_gather_rel(columns[i * chunk:(i + 1) * chunk], "col", n_col) for i in range(N_CHUNK)],
        axis=0)
    n_pos = gathered.shape[0]
    ff_blk = up_weight.shape[1]
    quarter = ff_blk // n_row

    def up_block(d):
        w = lax.dynamic_slice_in_dim(up_weight, (r ^ d) * quarter, quarter, 1)
        return jnp.dot(gathered, w, precision=lax.Precision.HIGH,
                       preferred_element_type=jnp.float32)

    held = {d: lax.optimization_barrier(up_block(d)) for d in range(n_row)}
    flip = 1
    while flip < n_row:
        sent = [d for d in sorted(held) if d & flip]
        got = lax.ppermute(jnp.stack([held[d] for d in sent]), "row", _pairs(n_row, flip))
        held = {d ^ flip: held[d ^ flip] + got[i] for i, d in enumerate(sent)}
        flip *= 2
    bias_q = lax.dynamic_slice_in_dim(up_bias, r * quarter, quarter)
    acts = {0: jax.nn.gelu(held[0] + bias_q[None, :], approximate=True)}
    acts[1] = lax.ppermute(acts[0], "row", _pairs(n_row, 1))
    flip = 2
    while flip < n_row:
        mine = sorted(d for d in acts if d % 2 == 0)
        got = lax.ppermute(jnp.stack([acts[d] for d in mine]), "row", _pairs(n_row, flip))
        for i, d in enumerate(mine):
            acts[d ^ flip] = got[i]
        flip *= 2
    core = r % 2

    def down_pair(d):
        lo, hi = acts[d], acts[d ^ 1]
        pair = jnp.where(core == 0, jnp.concatenate([lo, hi], axis=1),
                         jnp.concatenate([hi, lo], axis=1))
        w = lax.dynamic_slice_in_dim(down_weight, ((r ^ d) // 2) * 2 * quarter, 2 * quarter, 0)
        return jnp.dot(pair, w, precision=lax.Precision.HIGH,
                       preferred_element_type=jnp.float32)

    partial_out = down_pair(0)
    far = sorted(d for d in acts if d % 2 == 0 and d != 0)
    if far:
        stacked, partial_out = lax.optimization_barrier(
            (jnp.stack([acts[d] for d in far]), partial_out))
        got = lax.ppermute(stacked, "row", _pairs(n_row, 1))
        for i, d in enumerate(far):
            acts[d ^ 1] = got[i]
        for d in far:
            partial_out = partial_out + down_pair(d)
    per_chunk = partial_out.shape[0] // N_CHUNK
    out_share = jnp.concatenate(
        [_scatter_rel(partial_out[i * per_chunk:(i + 1) * per_chunk], "col", n_col)
         for i in range(N_CHUNK)], axis=0)
    back = _exchange_abs(out_share.reshape(n_row, tok_dev, d_blk), "row", n_row, r)
    returned = back.swapaxes(0, 1).reshape(tok_dev, n_row * d_blk)
    return tokens + gate_vec * (returned + down_bias)


def solution(mesh):
    in_specs = (
        P(("groups", "row", "col"), None),
        P(None, "groups", None),
        P("row", "col"),
        P("col"),
        P("col", "row"),
        P(),
    )
    out_specs = P(("groups", "row", "col"), None)
    return jax.shard_map(local, mesh=mesh, in_specs=in_specs, out_specs=out_specs, check_vma=False)
```

```python
import jax
import jax.numpy as jnp
from jax import lax
from jax.sharding import PartitionSpec as P

SEQ = 256
N_CHUNK = 2


layer_eps = 1e-06


def _pairs(n, flip):
    return [(i, i ^ flip) for i in range(n)]


def _gather_rel(x, axis, n):
    held = {0: x}
    flip = n // 2
    while flip >= 1:
        keys = sorted(held)
        got = lax.ppermute(jnp.stack([held[k] for k in keys]), axis, _pairs(n, flip))
        for i, k in enumerate(keys):
            held[k ^ flip] = got[i]
        flip //= 2
    return jnp.concatenate([held[d] for d in range(n)], axis=0)


def _scatter_rel(x, axis, n):
    blk = x.shape[0] // n
    held = {d: x[d * blk:(d + 1) * blk] for d in range(n)}
    flip = 1
    while flip < n:
        sent = [d for d in sorted(held) if d & flip]
        got = lax.ppermute(jnp.stack([held[d] for d in sent]), axis, _pairs(n, flip))
        held = {d ^ flip: held[d ^ flip] + got[i] for i, d in enumerate(sent)}
        flip *= 2
    return held[0]


def _exchange_abs(blocks, axis, n, idx):
    got = [blocks[idx]]
    for d in range(1, n):
        got.append(lax.ppermute(blocks[idx ^ d], axis, _pairs(n, d)))
    rel = jnp.stack(got)
    return jnp.stack([rel[s ^ idx] for s in range(n)])


def local(tokens, modulation, up_weight, up_bias, down_weight, down_bias):
    n_row = lax.axis_size("row")
    tok_dev = tokens.shape[0]
    first_tok = (lax.axis_index("row") * lax.axis_size("col") + lax.axis_index("col")) * tok_dev
    sample = first_tok // SEQ
    own_mods = lax.dynamic_slice_in_dim(modulation, sample, 1, 1)[:, 0]
    shift_vec = own_mods[0]
    scale_vec = own_mods[1]
    gate_vec = own_mods[2]
    average = jnp.mean(tokens, axis=1, keepdims=True)
    centred = tokens - average
    spread_sq = jnp.mean(centred * centred, axis=1, keepdims=True)
    normed = centred * lax.rsqrt(spread_sq + layer_eps)
    mixed = normed * (1.0 + scale_vec) + shift_vec
    r = lax.axis_index("row")
    d_blk = mixed.shape[1] // n_row
    sent_in = mixed.reshape(tok_dev, n_row, d_blk).swapaxes(0, 1)
    columns = _exchange_abs(sent_in, "row", n_row, r).reshape(n_row * tok_dev, d_blk)
    n_col = lax.axis_size("col")
    chunk = columns.shape[0] // N_CHUNK
    gathered = jnp.concatenate(
        [_gather_rel(columns[i * chunk:(i + 1) * chunk], "col", n_col) for i in range(N_CHUNK)],
        axis=0)
    n_pos = gathered.shape[0]
    ff_blk = up_weight.shape[1]
    quarter = ff_blk // n_row

    def up_block(d):
        w = lax.dynamic_slice_in_dim(up_weight, (r ^ d) * quarter, quarter, 1)
        return jnp.dot(gathered, w, precision=lax.Precision.HIGH,
                       preferred_element_type=jnp.float32)

    held = {d: lax.optimization_barrier(up_block(d)) for d in range(n_row)}
    flip = 1
    while flip < n_row:
        sent = [d for d in sorted(held) if d & flip]
        got = lax.ppermute(jnp.stack([held[d] for d in sent]), "row", _pairs(n_row, flip))
        held = {d ^ flip: held[d ^ flip] + got[i] for i, d in enumerate(sent)}
        flip *= 2
    bias_q = lax.dynamic_slice_in_dim(up_bias, r * quarter, quarter)
    acts = {0: jax.nn.gelu(held[0] + bias_q[None, :], approximate=True)}
    acts[1] = lax.ppermute(acts[0], "row", _pairs(n_row, 1))
    flip = 2
    while flip < n_row:
        mine = sorted(d for d in acts if d % 2 == 0)
        got = lax.ppermute(jnp.stack([acts[d] for d in mine]), "row", _pairs(n_row, flip))
        for i, d in enumerate(mine):
            acts[d ^ flip] = got[i]
        flip *= 2
    core = r % 2

    def down_pair(d, col0, cols):
        lo, hi = acts[d], acts[d ^ 1]
        pair = jnp.where(core == 0, jnp.concatenate([lo, hi], axis=1),
                         jnp.concatenate([hi, lo], axis=1))
        w = lax.dynamic_slice(down_weight, (((r ^ d) // 2) * 2 * quarter, col0),
                              (2 * quarter, cols))
        return jnp.dot(pair, w, precision=lax.Precision.HIGH,
                       preferred_element_type=jnp.float32)

    d_cols = down_weight.shape[1]
    partial_out = down_pair(0, 0, d_cols)
    far = sorted(d for d in acts if d % 2 == 0 and d != 0)
    if far:
        stacked, partial_out = lax.optimization_barrier(
            (jnp.stack([acts[d] for d in far]), partial_out))
        got = lax.ppermute(stacked, "row", _pairs(n_row, 1))
        for i, d in enumerate(far):
            acts[d ^ 1] = got[i]
    half = d_cols // 2
    halves = []
    for h in range(2):
        part = partial_out[:, h * half:(h + 1) * half]
        for d in far:
            part = part + down_pair(d, h * half, half)
        halves.append(part)
    per_chunk = n_pos // N_CHUNK
    out_share = jnp.concatenate(
        [jnp.concatenate([_scatter_rel(hv[i * per_chunk:(i + 1) * per_chunk], "col", n_col)
                          for hv in halves], axis=1)
         for i in range(N_CHUNK)], axis=0)
    back = _exchange_abs(out_share.reshape(n_row, tok_dev, d_blk), "row", n_row, r)
    returned = back.swapaxes(0, 1).reshape(tok_dev, n_row * d_blk)
    return tokens + gate_vec * (returned + down_bias)


def solution(mesh):
    in_specs = (
        P(("groups", "row", "col"), None),
        P(None, "groups", None),
        P("row", "col"),
        P("col"),
        P("col", "row"),
        P(),
    )
    out_specs = P(("groups", "row", "col"), None)
    return jax.shard_map(local, mesh=mesh, in_specs=in_specs, out_specs=out_specs, check_vma=False)
```

```python
import jax
import jax.numpy as jnp
from jax import lax
from jax.sharding import PartitionSpec as P
from jax.experimental import pallas as pl
from jax.experimental.pallas import tpu as pltpu

SEQ = 256
N_CHUNK = 2


layer_eps = 1e-06


def _pairs(n, flip):
    return [(i, i ^ flip) for i in range(n)]


def _gather_rel(x, axis, n):
    held = {0: x}
    flip = n // 2
    while flip >= 1:
        keys = sorted(held)
        got = lax.ppermute(jnp.stack([held[k] for k in keys]), axis, _pairs(n, flip))
        for i, k in enumerate(keys):
            held[k ^ flip] = got[i]
        flip //= 2
    return jnp.concatenate([held[d] for d in range(n)], axis=0)


def _scatter_rel(x, axis, n):
    blk = x.shape[0] // n
    held = {d: x[d * blk:(d + 1) * blk] for d in range(n)}
    flip = 1
    while flip < n:
        sent = [d for d in sorted(held) if d & flip]
        got = lax.ppermute(jnp.stack([held[d] for d in sent]), axis, _pairs(n, flip))
        held = {d ^ flip: held[d ^ flip] + got[i] for i, d in enumerate(sent)}
        flip *= 2
    return held[0]


def _exchange_abs(blocks, axis, n, idx):
    got = [blocks[idx]]
    for d in range(1, n):
        got.append(lax.ppermute(blocks[idx ^ d], axis, _pairs(n, d)))
    rel = jnp.stack(got)
    return jnp.stack([rel[s ^ idx] for s in range(n)])


def _norm_kernel(x_ref, m_ref, o_ref):
    x = x_ref[...]
    average = jnp.mean(x, axis=1, keepdims=True)
    centred = x - average
    spread_sq = jnp.mean(centred * centred, axis=1, keepdims=True)
    normed = centred * lax.rsqrt(spread_sq + layer_eps)
    o_ref[...] = normed * (1.0 + m_ref[1:2, :]) + m_ref[0:1, :]


def _norm_modulate(tokens, mods):
    rows, width = tokens.shape
    return pl.pallas_call(
        _norm_kernel,
        out_shape=jax.ShapeDtypeStruct(tokens.shape, jnp.float32),
        in_specs=[pl.BlockSpec(memory_space=pltpu.VMEM)] * 2,
        out_specs=pl.BlockSpec(memory_space=pltpu.VMEM),
        cost_estimate=pl.CostEstimate(flops=8 * rows * width, transcendentals=rows,
                                      bytes_accessed=4 * (2 * rows + 3) * width),
    )(tokens, mods)


def local(tokens, modulation, up_weight, up_bias, down_weight, down_bias):
    n_row = lax.axis_size("row")
    tok_dev = tokens.shape[0]
    first_tok = (lax.axis_index("row") * lax.axis_size("col") + lax.axis_index("col")) * tok_dev
    sample = first_tok // SEQ
    own_mods = lax.dynamic_slice_in_dim(modulation, sample, 1, 1)[:, 0]
    gate_vec = own_mods[2]
    mixed = _norm_modulate(tokens, own_mods)
    r = lax.axis_index("row")
    d_blk = mixed.shape[1] // n_row
    sent_in = mixed.reshape(tok_dev, n_row, d_blk).swapaxes(0, 1)
    columns = _exchange_abs(sent_in, "row", n_row, r).reshape(n_row * tok_dev, d_blk)
    n_col = lax.axis_size("col")
    chunk = columns.shape[0] // N_CHUNK
    gathered = jnp.concatenate(
        [_gather_rel(columns[i * chunk:(i + 1) * chunk], "col", n_col) for i in range(N_CHUNK)],
        axis=0)
    n_pos = gathered.shape[0]
    ff_blk = up_weight.shape[1]
    quarter = ff_blk // n_row

    def up_block(d):
        w = lax.dynamic_slice_in_dim(up_weight, (r ^ d) * quarter, quarter, 1)
        return jnp.dot(gathered, w, precision=lax.Precision.HIGH,
                       preferred_element_type=jnp.float32)

    held = {d: lax.optimization_barrier(up_block(d)) for d in range(n_row)}
    flip = 1
    while flip < n_row:
        sent = [d for d in sorted(held) if d & flip]
        got = lax.ppermute(jnp.stack([held[d] for d in sent]), "row", _pairs(n_row, flip))
        held = {d ^ flip: held[d ^ flip] + got[i] for i, d in enumerate(sent)}
        flip *= 2
    bias_q = lax.dynamic_slice_in_dim(up_bias, r * quarter, quarter)
    acts = {0: jax.nn.gelu(held[0] + bias_q[None, :], approximate=True)}
    acts[1] = lax.ppermute(acts[0], "row", _pairs(n_row, 1))
    flip = 2
    while flip < n_row:
        mine = sorted(d for d in acts if d % 2 == 0)
        got = lax.ppermute(jnp.stack([acts[d] for d in mine]), "row", _pairs(n_row, flip))
        for i, d in enumerate(mine):
            acts[d ^ flip] = got[i]
        flip *= 2
    core = r % 2

    def down_pair(d):
        lo, hi = acts[d], acts[d ^ 1]
        pair = jnp.where(core == 0, jnp.concatenate([lo, hi], axis=1),
                         jnp.concatenate([hi, lo], axis=1))
        w = lax.dynamic_slice_in_dim(down_weight, ((r ^ d) // 2) * 2 * quarter, 2 * quarter, 0)
        return jnp.dot(pair, w, precision=lax.Precision.HIGH,
                       preferred_element_type=jnp.float32)

    partial_out = down_pair(0)
    far = sorted(d for d in acts if d % 2 == 0 and d != 0)
    if far:
        stacked, partial_out = lax.optimization_barrier(
            (jnp.stack([acts[d] for d in far]), partial_out))
        got = lax.ppermute(stacked, "row", _pairs(n_row, 1))
        for i, d in enumerate(far):
            acts[d ^ 1] = got[i]
        for d in far:
            partial_out = partial_out + down_pair(d)
    per_chunk = partial_out.shape[0] // N_CHUNK
    out_share = jnp.concatenate(
        [_scatter_rel(partial_out[i * per_chunk:(i + 1) * per_chunk], "col", n_col)
         for i in range(N_CHUNK)], axis=0)
    back = _exchange_abs(out_share.reshape(n_row, tok_dev, d_blk), "row", n_row, r)
    returned = back.swapaxes(0, 1).reshape(tok_dev, n_row * d_blk)
    return tokens + gate_vec * (returned + down_bias)


def solution(mesh):
    in_specs = (
        P(("groups", "row", "col"), None),
        P(None, "groups", None),
        P("row", "col"),
        P("col"),
        P("col", "row"),
        P(),
    )
    out_specs = P(("groups", "row", "col"), None)
    return jax.shard_map(local, mesh=mesh, in_specs=in_specs, out_specs=out_specs, check_vma=False)
```

```python
import jax
import jax.numpy as jnp
from jax import lax
from jax.sharding import PartitionSpec as P

SEQ = 256
N_CHUNK = 2


layer_eps = 1e-06


def _pairs(n, flip):
    return [(i, i ^ flip) for i in range(n)]


def _gather_rel(x, axis, n):
    held = {0: x}
    flip = n // 2
    while flip >= 1:
        keys = sorted(held)
        got = lax.ppermute(jnp.stack([held[k] for k in keys]), axis, _pairs(n, flip))
        for i, k in enumerate(keys):
            held[k ^ flip] = got[i]
        flip //= 2
    return jnp.concatenate([held[d] for d in range(n)], axis=0)


def _scatter_rel(x, axis, n):
    blk = x.shape[0] // n
    held = {d: x[d * blk:(d + 1) * blk] for d in range(n)}
    flip = 1
    while flip < n:
        sent = [d for d in sorted(held) if d & flip]
        got = lax.ppermute(jnp.stack([held[d] for d in sent]), axis, _pairs(n, flip))
        held = {d ^ flip: held[d ^ flip] + got[i] for i, d in enumerate(sent)}
        flip *= 2
    return held[0]


def _exchange_abs(blocks, axis, n, idx):
    got = [blocks[idx]]
    for d in range(1, n):
        got.append(lax.ppermute(blocks[idx ^ d], axis, _pairs(n, d)))
    rel = jnp.stack(got)
    return jnp.stack([rel[s ^ idx] for s in range(n)])


def local(tokens, modulation, up_weight, up_bias, down_weight, down_bias):
    n_row = lax.axis_size("row")
    tok_dev = tokens.shape[0]
    first_tok = (lax.axis_index("row") * lax.axis_size("col") + lax.axis_index("col")) * tok_dev
    sample = first_tok // SEQ
    own_mods = lax.dynamic_slice_in_dim(modulation, sample, 1, 1)[:, 0]
    shift_vec = own_mods[0]
    scale_vec = own_mods[1]
    gate_vec = own_mods[2]
    average = jnp.mean(tokens, axis=1, keepdims=True)
    centred = tokens - average
    spread_sq = jnp.mean(centred * centred, axis=1, keepdims=True)
    normed = centred * lax.rsqrt(spread_sq + layer_eps)
    mixed = normed * (1.0 + scale_vec) + shift_vec
    r = lax.axis_index("row")
    d_blk = mixed.shape[1] // n_row
    sent_in = mixed.reshape(tok_dev, n_row, d_blk).swapaxes(0, 1)
    columns = _exchange_abs(sent_in, "row", n_row, r).reshape(n_row * tok_dev, d_blk)
    n_col = lax.axis_size("col")
    chunk = columns.shape[0] // N_CHUNK
    gathered = jnp.concatenate(
        [_gather_rel(columns[i * chunk:(i + 1) * chunk], "col", n_col) for i in range(N_CHUNK)],
        axis=0)
    n_pos = gathered.shape[0]
    ff_blk = up_weight.shape[1]
    quarter = ff_blk // n_row

    def up_block(d, lhs):
        w = lax.dynamic_slice_in_dim(up_weight, (r ^ d) * quarter, quarter, 1)
        return jnp.dot(lhs, w, precision=lax.Precision.HIGH,
                       preferred_element_type=jnp.float32)

    def low_bit(d):
        return (d & -d) if d else 2 * n_row

    odd = sorted(range(1, n_row, 2), key=lambda d: low_bit(d ^ 1))
    even = sorted(range(0, n_row, 2), key=low_bit)
    recv = {}
    held = {}
    lhs = gathered
    for d_odd, d_even in zip(odd, even):
        recv[d_odd ^ 1] = lax.ppermute(
            lax.optimization_barrier(up_block(d_odd, lhs)), "row", _pairs(n_row, 1))
        held[d_even] = lax.optimization_barrier(up_block(d_even, lhs)) + recv[d_even]
        if d_even == even[0]:
            lhs, held[d_even] = lax.optimization_barrier((lhs, held[d_even]))
    flip = 2
    while flip < n_row:
        sent = [d for d in sorted(held) if d & flip]
        got = lax.ppermute(jnp.stack([held[d] for d in sent]), "row", _pairs(n_row, flip))
        held = {d ^ flip: held[d ^ flip] + got[i] for i, d in enumerate(sent)}
        flip *= 2
    bias_q = lax.dynamic_slice_in_dim(up_bias, r * quarter, quarter)
    acts = {0: jax.nn.gelu(held[0] + bias_q[None, :], approximate=True)}
    acts[1] = lax.ppermute(acts[0], "row", _pairs(n_row, 1))
    flip = 2
    while flip < n_row:
        mine = sorted(d for d in acts if d % 2 == 0)
        got = lax.ppermute(jnp.stack([acts[d] for d in mine]), "row", _pairs(n_row, flip))
        for i, d in enumerate(mine):
            acts[d ^ flip] = got[i]
        flip *= 2
    core = r % 2

    def down_pair(d):
        lo, hi = acts[d], acts[d ^ 1]
        pair = jnp.where(core == 0, jnp.concatenate([lo, hi], axis=1),
                         jnp.concatenate([hi, lo], axis=1))
        w = lax.dynamic_slice_in_dim(down_weight, ((r ^ d) // 2) * 2 * quarter, 2 * quarter, 0)
        return jnp.dot(pair, w, precision=lax.Precision.HIGH,
                       preferred_element_type=jnp.float32)

    partial_out = down_pair(0)
    far = sorted(d for d in acts if d % 2 == 0 and d != 0)
    if far:
        stacked, partial_out = lax.optimization_barrier(
            (jnp.stack([acts[d] for d in far]), partial_out))
        got = lax.ppermute(stacked, "row", _pairs(n_row, 1))
        for i, d in enumerate(far):
            acts[d ^ 1] = got[i]
        for d in far:
            partial_out = partial_out + down_pair(d)
    per_chunk = partial_out.shape[0] // N_CHUNK
    out_share = jnp.concatenate(
        [_scatter_rel(partial_out[i * per_chunk:(i + 1) * per_chunk], "col", n_col)
         for i in range(N_CHUNK)], axis=0)
    back = _exchange_abs(out_share.reshape(n_row, tok_dev, d_blk), "row", n_row, r)
    returned = back.swapaxes(0, 1).reshape(tok_dev, n_row * d_blk)
    return tokens + gate_vec * (returned + down_bias)


def solution(mesh):
    in_specs = (
        P(("groups", "row", "col"), None),
        P(None, "groups", None),
        P("row", "col"),
        P("col"),
        P("col", "row"),
        P(),
    )
    out_specs = P(("groups", "row", "col"), None)
    return jax.shard_map(local, mesh=mesh, in_specs=in_specs, out_specs=out_specs, check_vma=False)
```

```python
import jax
import jax.numpy as jnp
from jax import lax
from jax.sharding import PartitionSpec as P

SEQ = 256
N_CHUNK = 4


layer_eps = 1e-06


def _pairs(n, flip):
    return [(i, i ^ flip) for i in range(n)]


def _gather_rel(x, axis, n):
    held = {0: x}
    flip = n // 2
    while flip >= 1:
        keys = sorted(held)
        got = lax.ppermute(jnp.stack([held[k] for k in keys]), axis, _pairs(n, flip))
        for i, k in enumerate(keys):
            held[k ^ flip] = got[i]
        flip //= 2
    return jnp.concatenate([held[d] for d in range(n)], axis=0)


def _scatter_rel(x, axis, n):
    blk = x.shape[0] // n
    held = {d: x[d * blk:(d + 1) * blk] for d in range(n)}
    flip = 1
    while flip < n:
        sent = [d for d in sorted(held) if d & flip]
        got = lax.ppermute(jnp.stack([held[d] for d in sent]), axis, _pairs(n, flip))
        held = {d ^ flip: held[d ^ flip] + got[i] for i, d in enumerate(sent)}
        flip *= 2
    return held[0]


def _exchange_abs(blocks, axis, n, idx):
    got = [blocks[idx]]
    for d in range(1, n):
        got.append(lax.ppermute(blocks[idx ^ d], axis, _pairs(n, d)))
    rel = jnp.stack(got)
    return jnp.stack([rel[s ^ idx] for s in range(n)])


def local(tokens, modulation, up_weight, up_bias, down_weight, down_bias):
    n_row = lax.axis_size("row")
    tok_dev = tokens.shape[0]
    first_tok = (lax.axis_index("row") * lax.axis_size("col") + lax.axis_index("col")) * tok_dev
    sample = first_tok // SEQ
    own_mods = lax.dynamic_slice_in_dim(modulation, sample, 1, 1)[:, 0]
    shift_vec = own_mods[0]
    scale_vec = own_mods[1]
    gate_vec = own_mods[2]
    average = jnp.mean(tokens, axis=1, keepdims=True)
    centred = tokens - average
    spread_sq = jnp.mean(centred * centred, axis=1, keepdims=True)
    normed = centred * lax.rsqrt(spread_sq + layer_eps)
    mixed = normed * (1.0 + scale_vec) + shift_vec
    r = lax.axis_index("row")
    d_blk = mixed.shape[1] // n_row
    sent_in = mixed.reshape(tok_dev, n_row, d_blk).swapaxes(0, 1)
    columns = _exchange_abs(sent_in, "row", n_row, r).reshape(n_row * tok_dev, d_blk)
    n_col = lax.axis_size("col")
    chunk = columns.shape[0] // N_CHUNK
    gathered = jnp.concatenate(
        [_gather_rel(columns[i * chunk:(i + 1) * chunk], "col", n_col) for i in range(N_CHUNK)],
        axis=0)
    n_pos = gathered.shape[0]
    ff_blk = up_weight.shape[1]
    quarter = ff_blk // n_row

    def up_block(d, lhs):
        w = lax.dynamic_slice_in_dim(up_weight, (r ^ d) * quarter, quarter, 1)
        return jnp.dot(lhs, w, precision=lax.Precision.HIGH,
                       preferred_element_type=jnp.float32)

    def low_bit(d):
        return (d & -d) if d else 2 * n_row

    odd = sorted(range(1, n_row, 2), key=lambda d: low_bit(d ^ 1))
    even = sorted(range(0, n_row, 2), key=low_bit)
    recv = {}
    held = {}
    lhs = gathered
    for d_odd, d_even in zip(odd, even):
        recv[d_odd ^ 1] = lax.ppermute(
            lax.optimization_barrier(up_block(d_odd, lhs)), "row", _pairs(n_row, 1))
        held[d_even] = lax.optimization_barrier(up_block(d_even, lhs)) + recv[d_even]
        if d_even == even[0]:
            lhs, held[d_even] = lax.optimization_barrier((lhs, held[d_even]))
    flip = 2
    while flip < n_row:
        sent = [d for d in sorted(held) if d & flip]
        got = lax.ppermute(jnp.stack([held[d] for d in sent]), "row", _pairs(n_row, flip))
        held = {d ^ flip: held[d ^ flip] + got[i] for i, d in enumerate(sent)}
        flip *= 2
    bias_q = lax.dynamic_slice_in_dim(up_bias, r * quarter, quarter)
    acts = {0: jax.nn.gelu(held[0] + bias_q[None, :], approximate=True)}
    acts[1] = lax.ppermute(acts[0], "row", _pairs(n_row, 1))
    flip = 2
    while flip < n_row:
        mine = sorted(d for d in acts if d % 2 == 0)
        got = lax.ppermute(jnp.stack([acts[d] for d in mine]), "row", _pairs(n_row, flip))
        for i, d in enumerate(mine):
            acts[d ^ flip] = got[i]
        flip *= 2
    core = r % 2

    def down_pair(d):
        lo, hi = acts[d], acts[d ^ 1]
        pair = jnp.where(core == 0, jnp.concatenate([lo, hi], axis=1),
                         jnp.concatenate([hi, lo], axis=1))
        w = lax.dynamic_slice_in_dim(down_weight, ((r ^ d) // 2) * 2 * quarter, 2 * quarter, 0)
        return jnp.dot(pair, w, precision=lax.Precision.HIGH,
                       preferred_element_type=jnp.float32)

    partial_out = down_pair(0)
    far = sorted(d for d in acts if d % 2 == 0 and d != 0)
    if far:
        stacked, partial_out = lax.optimization_barrier(
            (jnp.stack([acts[d] for d in far]), partial_out))
        got = lax.ppermute(stacked, "row", _pairs(n_row, 1))
        for i, d in enumerate(far):
            acts[d ^ 1] = got[i]
        for d in far:
            partial_out = partial_out + down_pair(d)
    per_chunk = partial_out.shape[0] // N_CHUNK
    out_share = jnp.concatenate(
        [_scatter_rel(partial_out[i * per_chunk:(i + 1) * per_chunk], "col", n_col)
         for i in range(N_CHUNK)], axis=0)
    back = _exchange_abs(out_share.reshape(n_row, tok_dev, d_blk), "row", n_row, r)
    returned = back.swapaxes(0, 1).reshape(tok_dev, n_row * d_blk)
    return tokens + gate_vec * (returned + down_bias)


def solution(mesh):
    in_specs = (
        P(("groups", "row", "col"), None),
        P(None, "groups", None),
        P("row", "col"),
        P("col"),
        P("col", "row"),
        P(),
    )
    out_specs = P(("groups", "row", "col"), None)
    return jax.shard_map(local, mesh=mesh, in_specs=in_specs, out_specs=out_specs, check_vma=False)
```

```python
import jax
import jax.numpy as jnp
from jax import lax
from jax.sharding import PartitionSpec as P

SEQ = 256
N_CHUNK = 2


layer_eps = 1e-06


def _pairs(n, flip):
    return [(i, i ^ flip) for i in range(n)]


def _gather_rel(x, axis, n):
    held = {0: x}
    flip = n // 2
    while flip >= 1:
        keys = sorted(held)
        got = lax.ppermute(jnp.stack([held[k] for k in keys]), axis, _pairs(n, flip))
        for i, k in enumerate(keys):
            held[k ^ flip] = got[i]
        flip //= 2
    return jnp.concatenate([held[d] for d in range(n)], axis=0)


def _scatter_rel(x, axis, n):
    blk = x.shape[0] // n
    held = {d: x[d * blk:(d + 1) * blk] for d in range(n)}
    flip = 1
    while flip < n:
        sent = [d for d in sorted(held) if d & flip]
        got = lax.ppermute(jnp.stack([held[d] for d in sent]), axis, _pairs(n, flip))
        held = {d ^ flip: held[d ^ flip] + got[i] for i, d in enumerate(sent)}
        flip *= 2
    return held[0]


def _exchange_abs(blocks, axis, n, idx):
    got = [blocks[idx]]
    for d in range(1, n):
        got.append(lax.ppermute(blocks[idx ^ d], axis, _pairs(n, d)))
    rel = jnp.stack(got)
    return jnp.stack([rel[s ^ idx] for s in range(n)])


def local(tokens, modulation, up_weight, up_bias, down_weight, down_bias):
    n_row = lax.axis_size("row")
    tok_dev = tokens.shape[0]
    first_tok = (lax.axis_index("row") * lax.axis_size("col") + lax.axis_index("col")) * tok_dev
    sample = first_tok // SEQ
    own_mods = lax.dynamic_slice_in_dim(modulation, sample, 1, 1)[:, 0]
    shift_vec = own_mods[0]
    scale_vec = own_mods[1]
    gate_vec = own_mods[2]
    average = jnp.mean(tokens, axis=1, keepdims=True)
    centred = tokens - average
    spread_sq = jnp.mean(centred * centred, axis=1, keepdims=True)
    normed = centred * lax.rsqrt(spread_sq + layer_eps)
    mixed = normed * (1.0 + scale_vec) + shift_vec
    r = lax.axis_index("row")
    d_blk = mixed.shape[1] // n_row
    sent_in = mixed.reshape(tok_dev, n_row, d_blk).swapaxes(0, 1)
    columns = _exchange_abs(sent_in, "row", n_row, r).reshape(n_row * tok_dev, d_blk)
    n_col = lax.axis_size("col")
    chunk = columns.shape[0] // N_CHUNK
    gathered = jnp.concatenate(
        [_gather_rel(columns[i * chunk:(i + 1) * chunk], "col", n_col) for i in range(N_CHUNK)],
        axis=0)
    n_pos = gathered.shape[0]
    ff_blk = up_weight.shape[1]
    quarter = ff_blk // n_row

    def up_block(d, lhs):
        w = lax.dynamic_slice_in_dim(up_weight, (r ^ d) * quarter, quarter, 1)
        return jnp.dot(lhs, w, precision=lax.Precision.HIGH,
                       preferred_element_type=jnp.float32)

    def low_bit(d):
        return (d & -d) if d else 2 * n_row

    core = r % 2

    def up_pair(d, lhs):
        w = lax.dynamic_slice_in_dim(up_weight, ((r ^ d) // 2) * 2 * quarter, 2 * quarter, 1)
        both = lax.optimization_barrier(
            jnp.dot(lhs, w, precision=lax.Precision.HIGH,
                    preferred_element_type=jnp.float32))
        mine = lax.dynamic_slice_in_dim(both, core * quarter, quarter, 1)
        other = lax.dynamic_slice_in_dim(both, (1 - core) * quarter, quarter, 1)
        return mine, other

    held = {}
    lhs = gathered
    for i, d_even in enumerate(sorted(range(0, n_row, 2), key=low_bit)):
        if d_even:
            mine, other = up_pair(d_even, lhs)
        else:
            other = lax.optimization_barrier(up_block(1, lhs))
            mine = lax.optimization_barrier(up_block(0, lhs))
        held[d_even] = mine + lax.ppermute(other, "row", _pairs(n_row, 1))
        if i == 0:
            lhs, held[d_even] = lax.optimization_barrier((lhs, held[d_even]))
    flip = 2
    while flip < n_row:
        sent = [d for d in sorted(held) if d & flip]
        got = lax.ppermute(jnp.stack([held[d] for d in sent]), "row", _pairs(n_row, flip))
        held = {d ^ flip: held[d ^ flip] + got[i] for i, d in enumerate(sent)}
        flip *= 2
    bias_q = lax.dynamic_slice_in_dim(up_bias, r * quarter, quarter)
    acts = {0: jax.nn.gelu(held[0] + bias_q[None, :], approximate=True)}
    acts[1] = lax.ppermute(acts[0], "row", _pairs(n_row, 1))
    flip = 2
    while flip < n_row:
        mine = sorted(d for d in acts if d % 2 == 0)
        got = lax.ppermute(jnp.stack([acts[d] for d in mine]), "row", _pairs(n_row, flip))
        for i, d in enumerate(mine):
            acts[d ^ flip] = got[i]
        flip *= 2

    def down_pair(d):
        lo, hi = acts[d], acts[d ^ 1]
        pair = jnp.where(core == 0, jnp.concatenate([lo, hi], axis=1),
                         jnp.concatenate([hi, lo], axis=1))
        w = lax.dynamic_slice_in_dim(down_weight, ((r ^ d) // 2) * 2 * quarter, 2 * quarter, 0)
        return jnp.dot(pair, w, precision=lax.Precision.HIGH,
                       preferred_element_type=jnp.float32)

    partial_out = down_pair(0)
    far = sorted(d for d in acts if d % 2 == 0 and d != 0)
    if far:
        stacked, partial_out = lax.optimization_barrier(
            (jnp.stack([acts[d] for d in far]), partial_out))
        got = lax.ppermute(stacked, "row", _pairs(n_row, 1))
        for i, d in enumerate(far):
            acts[d ^ 1] = got[i]
        for d in far:
            partial_out = partial_out + down_pair(d)
    per_chunk = partial_out.shape[0] // N_CHUNK
    out_share = jnp.concatenate(
        [_scatter_rel(partial_out[i * per_chunk:(i + 1) * per_chunk], "col", n_col)
         for i in range(N_CHUNK)], axis=0)
    back = _exchange_abs(out_share.reshape(n_row, tok_dev, d_blk), "row", n_row, r)
    returned = back.swapaxes(0, 1).reshape(tok_dev, n_row * d_blk)
    return tokens + gate_vec * (returned + down_bias)


def solution(mesh):
    in_specs = (
        P(("groups", "row", "col"), None),
        P(None, "groups", None),
        P("row", "col"),
        P("col"),
        P("col", "row"),
        P(),
    )
    out_specs = P(("groups", "row", "col"), None)
    return jax.shard_map(local, mesh=mesh, in_specs=in_specs, out_specs=out_specs, check_vma=False)
```

```python
import jax
import jax.numpy as jnp
from jax import lax
from jax.sharding import PartitionSpec as P
from jax.experimental import pallas as pl
from jax.experimental.pallas import tpu as pltpu

SEQ = 256
N_CHUNK = 2


layer_eps = 1e-06


def _pairs(n, flip):
    return [(i, i ^ flip) for i in range(n)]


def _gather_rel(x, axis, n):
    held = {0: x}
    flip = n // 2
    while flip >= 1:
        keys = sorted(held)
        got = lax.ppermute(jnp.stack([held[k] for k in keys]), axis, _pairs(n, flip))
        for i, k in enumerate(keys):
            held[k ^ flip] = got[i]
        flip //= 2
    return jnp.concatenate([held[d] for d in range(n)], axis=0)


def _scatter_rel(x, axis, n):
    blk = x.shape[0] // n
    held = {d: x[d * blk:(d + 1) * blk] for d in range(n)}
    flip = 1
    while flip < n:
        sent = [d for d in sorted(held) if d & flip]
        got = lax.ppermute(jnp.stack([held[d] for d in sent]), axis, _pairs(n, flip))
        held = {d ^ flip: held[d ^ flip] + got[i] for i, d in enumerate(sent)}
        flip *= 2
    return held[0]


def _exchange_abs(blocks, axis, n, idx):
    got = [blocks[idx]]
    for d in range(1, n):
        got.append(lax.ppermute(blocks[idx ^ d], axis, _pairs(n, d)))
    rel = jnp.stack(got)
    return jnp.stack([rel[s ^ idx] for s in range(n)])


def _norm_kernel(x_ref, o_ref):
    x = x_ref[...]
    average = jnp.mean(x, axis=1, keepdims=True)
    centred = x - average
    spread_sq = jnp.mean(centred * centred, axis=1, keepdims=True)
    o_ref[...] = centred * lax.rsqrt(spread_sq + layer_eps)


def _normalize(tokens):
    rows, width = tokens.shape
    return pl.pallas_call(
        _norm_kernel,
        out_shape=jax.ShapeDtypeStruct(tokens.shape, jnp.float32),
        in_specs=[pl.BlockSpec(memory_space=pltpu.VMEM)],
        out_specs=pl.BlockSpec(memory_space=pltpu.VMEM),
        cost_estimate=pl.CostEstimate(flops=6 * rows * width, transcendentals=rows,
                                      bytes_accessed=8 * rows * width),
    )(tokens)


def local(tokens, modulation, up_weight, up_bias, down_weight, down_bias):
    n_row = lax.axis_size("row")
    tok_dev = tokens.shape[0]
    first_tok = (lax.axis_index("row") * lax.axis_size("col") + lax.axis_index("col")) * tok_dev
    sample = first_tok // SEQ
    own_mods = lax.dynamic_slice_in_dim(modulation, sample, 1, 1)[:, 0]
    shift_vec = own_mods[0]
    scale_vec = own_mods[1]
    gate_vec = own_mods[2]
    normed = _normalize(tokens)
    mixed = normed * (1.0 + scale_vec) + shift_vec
    r = lax.axis_index("row")
    d_blk = mixed.shape[1] // n_row
    sent_in = mixed.reshape(tok_dev, n_row, d_blk).swapaxes(0, 1)
    columns = _exchange_abs(sent_in, "row", n_row, r).reshape(n_row * tok_dev, d_blk)
    n_col = lax.axis_size("col")
    chunk = columns.shape[0] // N_CHUNK
    gathered = jnp.concatenate(
        [_gather_rel(columns[i * chunk:(i + 1) * chunk], "col", n_col) for i in range(N_CHUNK)],
        axis=0)
    n_pos = gathered.shape[0]
    ff_blk = up_weight.shape[1]
    quarter = ff_blk // n_row

    def up_block(d, lhs):
        w = lax.dynamic_slice_in_dim(up_weight, (r ^ d) * quarter, quarter, 1)
        return jnp.dot(lhs, w, precision=lax.Precision.HIGH,
                       preferred_element_type=jnp.float32)

    def low_bit(d):
        return (d & -d) if d else 2 * n_row

    core = r % 2

    def up_pair(d, lhs):
        w = lax.dynamic_slice_in_dim(up_weight, ((r ^ d) // 2) * 2 * quarter, 2 * quarter, 1)
        both = lax.optimization_barrier(
            jnp.dot(lhs, w, precision=lax.Precision.HIGH,
                    preferred_element_type=jnp.float32))
        mine = lax.dynamic_slice_in_dim(both, core * quarter, quarter, 1)
        other = lax.dynamic_slice_in_dim(both, (1 - core) * quarter, quarter, 1)
        return mine, other

    held = {}
    lhs = gathered
    for i, d_even in enumerate(sorted(range(0, n_row, 2), key=low_bit)):
        if d_even:
            mine, other = up_pair(d_even, lhs)
        else:
            other = lax.optimization_barrier(up_block(1, lhs))
            mine = lax.optimization_barrier(up_block(0, lhs))
        held[d_even] = mine + lax.ppermute(other, "row", _pairs(n_row, 1))
        if i == 0:
            lhs, held[d_even] = lax.optimization_barrier((lhs, held[d_even]))
    flip = 2
    while flip < n_row:
        sent = [d for d in sorted(held) if d & flip]
        got = lax.ppermute(jnp.stack([held[d] for d in sent]), "row", _pairs(n_row, flip))
        held = {d ^ flip: held[d ^ flip] + got[i] for i, d in enumerate(sent)}
        flip *= 2
    bias_q = lax.dynamic_slice_in_dim(up_bias, r * quarter, quarter)
    acts = {0: jax.nn.gelu(held[0] + bias_q[None, :], approximate=True)}
    acts[1] = lax.ppermute(acts[0], "row", _pairs(n_row, 1))
    flip = 2
    while flip < n_row:
        mine = sorted(d for d in acts if d % 2 == 0)
        got = lax.ppermute(jnp.stack([acts[d] for d in mine]), "row", _pairs(n_row, flip))
        for i, d in enumerate(mine):
            acts[d ^ flip] = got[i]
        flip *= 2

    def down_pair(d):
        lo, hi = acts[d], acts[d ^ 1]
        pair = jnp.where(core == 0, jnp.concatenate([lo, hi], axis=1),
                         jnp.concatenate([hi, lo], axis=1))
        w = lax.dynamic_slice_in_dim(down_weight, ((r ^ d) // 2) * 2 * quarter, 2 * quarter, 0)
        return jnp.dot(pair, w, precision=lax.Precision.HIGH,
                       preferred_element_type=jnp.float32)

    partial_out = down_pair(0)
    far = sorted(d for d in acts if d % 2 == 0 and d != 0)
    if far:
        stacked, partial_out = lax.optimization_barrier(
            (jnp.stack([acts[d] for d in far]), partial_out))
        got = lax.ppermute(stacked, "row", _pairs(n_row, 1))
        for i, d in enumerate(far):
            acts[d ^ 1] = got[i]
        for d in far:
            partial_out = partial_out + down_pair(d)
    per_chunk = partial_out.shape[0] // N_CHUNK
    out_share = jnp.concatenate(
        [_scatter_rel(partial_out[i * per_chunk:(i + 1) * per_chunk], "col", n_col)
         for i in range(N_CHUNK)], axis=0)
    back = _exchange_abs(out_share.reshape(n_row, tok_dev, d_blk), "row", n_row, r)
    returned = back.swapaxes(0, 1).reshape(tok_dev, n_row * d_blk)
    return tokens + gate_vec * (returned + down_bias)


def solution(mesh):
    in_specs = (
        P(("groups", "row", "col"), None),
        P(None, "groups", None),
        P("row", "col"),
        P("col"),
        P("col", "row"),
        P(),
    )
    out_specs = P(("groups", "row", "col"), None)
    return jax.shard_map(local, mesh=mesh, in_specs=in_specs, out_specs=out_specs, check_vma=False)
```

```python
import jax
import jax.numpy as jnp
from jax import lax
from jax.sharding import PartitionSpec as P
from jax.experimental import pallas as pl
from jax.experimental.pallas import tpu as pltpu

SEQ = 256
N_CHUNK = 2


layer_eps = 1e-06


def _pairs(n, flip):
    return [(i, i ^ flip) for i in range(n)]


def _gather_rel(x, axis, n):
    held = {0: x}
    flip = n // 2
    while flip >= 1:
        keys = sorted(held)
        got = lax.ppermute(jnp.stack([held[k] for k in keys]), axis, _pairs(n, flip))
        for i, k in enumerate(keys):
            held[k ^ flip] = got[i]
        flip //= 2
    return jnp.concatenate([held[d] for d in range(n)], axis=0)


def _scatter_rel(x, axis, n):
    blk = x.shape[0] // n
    held = {d: x[d * blk:(d + 1) * blk] for d in range(n)}
    flip = 1
    while flip < n:
        sent = [d for d in sorted(held) if d & flip]
        got = lax.ppermute(jnp.stack([held[d] for d in sent]), axis, _pairs(n, flip))
        held = {d ^ flip: held[d ^ flip] + got[i] for i, d in enumerate(sent)}
        flip *= 2
    return held[0]


def _exchange_abs(blocks, axis, n, idx):
    got = [blocks[idx]]
    for d in range(1, n):
        got.append(lax.ppermute(blocks[idx ^ d], axis, _pairs(n, d)))
    rel = jnp.stack(got)
    return jnp.stack([rel[s ^ idx] for s in range(n)])


def _norm_kernel(x_ref, shift_ref, scale_ref, o_ref):
    x = x_ref[...]
    average = jnp.mean(x, axis=1, keepdims=True)
    centred = x - average
    spread_sq = jnp.mean(centred * centred, axis=1, keepdims=True)
    normed = centred * lax.rsqrt(spread_sq + layer_eps)
    o_ref[...] = normed * (1.0 + scale_ref[...]) + shift_ref[...]


def _normalize(tokens, shift, scale):
    rows, width = tokens.shape
    return pl.pallas_call(
        _norm_kernel,
        out_shape=jax.ShapeDtypeStruct(tokens.shape, jnp.float32),
        in_specs=[pl.BlockSpec(memory_space=pltpu.VMEM)] * 3,
        out_specs=pl.BlockSpec(memory_space=pltpu.VMEM),
        cost_estimate=pl.CostEstimate(flops=6 * rows * width, transcendentals=rows,
                                      bytes_accessed=8 * rows * width),
    )(tokens, shift, scale)


def local(tokens, modulation, up_weight, up_bias, down_weight, down_bias):
    n_row = lax.axis_size("row")
    tok_dev = tokens.shape[0]
    first_tok = (lax.axis_index("row") * lax.axis_size("col") + lax.axis_index("col")) * tok_dev
    sample = first_tok // SEQ
    own_mods = lax.dynamic_slice_in_dim(modulation, sample, 1, 1)[:, 0]
    gate_vec = own_mods[2]
    shift_row = lax.dynamic_slice_in_dim(modulation[0], sample, 1, 0)
    scale_row = lax.dynamic_slice_in_dim(modulation[1], sample, 1, 0)
    mixed = _normalize(tokens, shift_row, scale_row)
    r = lax.axis_index("row")
    d_blk = mixed.shape[1] // n_row
    sent_in = mixed.reshape(tok_dev, n_row, d_blk).swapaxes(0, 1)
    columns = _exchange_abs(sent_in, "row", n_row, r).reshape(n_row * tok_dev, d_blk)
    n_col = lax.axis_size("col")
    chunk = columns.shape[0] // N_CHUNK
    gathered = jnp.concatenate(
        [_gather_rel(columns[i * chunk:(i + 1) * chunk], "col", n_col) for i in range(N_CHUNK)],
        axis=0)
    n_pos = gathered.shape[0]
    ff_blk = up_weight.shape[1]
    quarter = ff_blk // n_row

    def up_block(d, lhs):
        w = lax.dynamic_slice_in_dim(up_weight, (r ^ d) * quarter, quarter, 1)
        return jnp.dot(lhs, w, precision=lax.Precision.HIGH,
                       preferred_element_type=jnp.float32)

    def low_bit(d):
        return (d & -d) if d else 2 * n_row

    core = r % 2

    def up_pair(d, lhs):
        w = lax.dynamic_slice_in_dim(up_weight, ((r ^ d) // 2) * 2 * quarter, 2 * quarter, 1)
        both = lax.optimization_barrier(
            jnp.dot(lhs, w, precision=lax.Precision.HIGH,
                    preferred_element_type=jnp.float32))
        mine = lax.dynamic_slice_in_dim(both, core * quarter, quarter, 1)
        other = lax.dynamic_slice_in_dim(both, (1 - core) * quarter, quarter, 1)
        return mine, other

    held = {}
    lhs = gathered
    for i, d_even in enumerate(sorted(range(0, n_row, 2), key=low_bit)):
        if d_even:
            mine, other = up_pair(d_even, lhs)
        else:
            other = lax.optimization_barrier(up_block(1, lhs))
            mine = lax.optimization_barrier(up_block(0, lhs))
        if not d_even:
            bias_q = lax.dynamic_slice_in_dim(up_bias, r * quarter, quarter)
            mine = lax.optimization_barrier(mine + bias_q[None, :])
        held[d_even] = mine + lax.ppermute(other, "row", _pairs(n_row, 1))
        if i == 0:
            lhs, held[d_even] = lax.optimization_barrier((lhs, held[d_even]))
    flip = 2
    while flip < n_row:
        sent = [d for d in sorted(held) if d & flip]
        got = lax.ppermute(jnp.stack([held[d] for d in sent]), "row", _pairs(n_row, flip))
        held = {d ^ flip: held[d ^ flip] + got[i] for i, d in enumerate(sent)}
        flip *= 2
    acts = {0: jax.nn.gelu(held[0], approximate=True)}
    acts[1] = lax.ppermute(acts[0], "row", _pairs(n_row, 1))
    flip = 2
    while flip < n_row:
        mine = sorted(d for d in acts if d % 2 == 0)
        got = lax.ppermute(jnp.stack([acts[d] for d in mine]), "row", _pairs(n_row, flip))
        for i, d in enumerate(mine):
            acts[d ^ flip] = got[i]
        flip *= 2

    def down_pair(d):
        lo, hi = acts[d], acts[d ^ 1]
        pair = jnp.where(core == 0, jnp.concatenate([lo, hi], axis=1),
                         jnp.concatenate([hi, lo], axis=1))
        w = lax.dynamic_slice_in_dim(down_weight, ((r ^ d) // 2) * 2 * quarter, 2 * quarter, 0)
        return jnp.dot(pair, w, precision=lax.Precision.HIGH,
                       preferred_element_type=jnp.float32)

    partial_out = down_pair(0)
    far = sorted(d for d in acts if d % 2 == 0 and d != 0)
    if far:
        stacked, partial_out = lax.optimization_barrier(
            (jnp.stack([acts[d] for d in far]), partial_out))
        got = lax.ppermute(stacked, "row", _pairs(n_row, 1))
        for i, d in enumerate(far):
            acts[d ^ 1] = got[i]
        for d in far:
            partial_out = partial_out + down_pair(d)
    per_chunk = partial_out.shape[0] // N_CHUNK
    out_share = jnp.concatenate(
        [_scatter_rel(partial_out[i * per_chunk:(i + 1) * per_chunk], "col", n_col)
         for i in range(N_CHUNK)], axis=0)
    back = _exchange_abs(out_share.reshape(n_row, tok_dev, d_blk), "row", n_row, r)
    returned = back.swapaxes(0, 1).reshape(tok_dev, n_row * d_blk)
    return tokens + gate_vec * (returned + down_bias)


def solution(mesh):
    in_specs = (
        P(("groups", "row", "col"), None),
        P(None, "groups", None),
        P("row", "col"),
        P("col"),
        P("col", "row"),
        P(),
    )
    out_specs = P(("groups", "row", "col"), None)
    return jax.shard_map(local, mesh=mesh, in_specs=in_specs, out_specs=out_specs, check_vma=False)
```

```python
import jax
import jax.numpy as jnp
from jax import lax
from jax.sharding import PartitionSpec as P
from jax.experimental import pallas as pl
from jax.experimental.pallas import tpu as pltpu

SEQ = 256
N_CHUNK = 2


layer_eps = 1e-06


def _pairs(n, flip):
    return [(i, i ^ flip) for i in range(n)]


def _gather_rel(x, axis, n):
    held = {0: x}
    flip = n // 2
    while flip >= 1:
        keys = sorted(held)
        got = lax.ppermute(jnp.stack([held[k] for k in keys]), axis, _pairs(n, flip))
        for i, k in enumerate(keys):
            held[k ^ flip] = got[i]
        flip //= 2
    return jnp.concatenate([held[d] for d in range(n)], axis=0)


def _scatter_rel(x, axis, n):
    blk = x.shape[0] // n
    held = {d: x[d * blk:(d + 1) * blk] for d in range(n)}
    flip = 1
    while flip < n:
        sent = [d for d in sorted(held) if d & flip]
        got = lax.ppermute(jnp.stack([held[d] for d in sent]), axis, _pairs(n, flip))
        held = {d ^ flip: held[d ^ flip] + got[i] for i, d in enumerate(sent)}
        flip *= 2
    return held[0]


def _exchange_abs(blocks, axis, n, idx):
    got = [blocks[idx]]
    for d in range(1, n):
        got.append(lax.ppermute(blocks[idx ^ d], axis, _pairs(n, d)))
    rel = jnp.stack(got)
    return jnp.stack([rel[s ^ idx] for s in range(n)])


def _norm_kernel(x_ref, o_ref):
    x = x_ref[...]
    average = jnp.mean(x, axis=1, keepdims=True)
    centred = x - average
    spread_sq = jnp.mean(centred * centred, axis=1, keepdims=True)
    o_ref[...] = centred * lax.rsqrt(spread_sq + layer_eps)


def _normalize(tokens):
    rows, width = tokens.shape
    return pl.pallas_call(
        _norm_kernel,
        out_shape=jax.ShapeDtypeStruct(tokens.shape, jnp.float32),
        in_specs=[pl.BlockSpec(memory_space=pltpu.VMEM)],
        out_specs=pl.BlockSpec(memory_space=pltpu.VMEM),
        cost_estimate=pl.CostEstimate(flops=6 * rows * width, transcendentals=rows,
                                      bytes_accessed=8 * rows * width),
    )(tokens)


def local(tokens, modulation, up_weight, up_bias, down_weight, down_bias):
    n_row = lax.axis_size("row")
    tok_dev = tokens.shape[0]
    first_tok = (lax.axis_index("row") * lax.axis_size("col") + lax.axis_index("col")) * tok_dev
    sample = first_tok // SEQ
    own_mods = lax.dynamic_slice_in_dim(modulation, sample, 1, 1)[:, 0]
    shift_vec = own_mods[0]
    scale_vec = own_mods[1]
    gate_vec = own_mods[2]
    normed = _normalize(tokens)
    mixed = normed * (1.0 + scale_vec) + shift_vec
    r = lax.axis_index("row")
    d_blk = mixed.shape[1] // n_row
    sent_in = mixed.reshape(tok_dev, n_row, d_blk).swapaxes(0, 1)
    columns = _exchange_abs(sent_in, "row", n_row, r).reshape(n_row * tok_dev, d_blk)
    n_col = lax.axis_size("col")
    chunk = columns.shape[0] // N_CHUNK
    gathered = jnp.concatenate(
        [_gather_rel(columns[i * chunk:(i + 1) * chunk], "col", n_col) for i in range(N_CHUNK)],
        axis=0)
    n_pos = gathered.shape[0]
    ff_blk = up_weight.shape[1]
    quarter = ff_blk // n_row

    def up_block(d, lhs):
        w = lax.dynamic_slice_in_dim(up_weight, (r ^ d) * quarter, quarter, 1)
        return jnp.dot(lhs, w, precision=lax.Precision.HIGH,
                       preferred_element_type=jnp.float32)

    def low_bit(d):
        return (d & -d) if d else 2 * n_row

    core = r % 2

    def up_pair(d, lhs):
        w = lax.dynamic_slice_in_dim(up_weight, ((r ^ d) // 2) * 2 * quarter, 2 * quarter, 1)
        both = lax.optimization_barrier(
            jnp.dot(lhs, w, precision=lax.Precision.HIGH,
                    preferred_element_type=jnp.float32))
        mine = lax.dynamic_slice_in_dim(both, core * quarter, quarter, 1)
        other = lax.dynamic_slice_in_dim(both, (1 - core) * quarter, quarter, 1)
        return mine, other

    held = {}
    lhs = gathered
    for i, d_even in enumerate(sorted(range(0, n_row, 2), key=low_bit)):
        if d_even:
            mine, other = up_pair(d_even, lhs)
        else:
            other = lax.optimization_barrier(up_block(1, lhs))
            mine = lax.optimization_barrier(up_block(0, lhs))
        held[d_even] = mine + lax.ppermute(other, "row", _pairs(n_row, 1))
    flip = 2
    while flip < n_row:
        sent = [d for d in sorted(held) if d & flip]
        got = lax.ppermute(jnp.stack([held[d] for d in sent]), "row", _pairs(n_row, flip))
        held = {d ^ flip: held[d ^ flip] + got[i] for i, d in enumerate(sent)}
        flip *= 2
    bias_q = lax.dynamic_slice_in_dim(up_bias, r * quarter, quarter)
    acts = {0: jax.nn.gelu(held[0] + bias_q[None, :], approximate=True)}
    acts[1] = lax.ppermute(acts[0], "row", _pairs(n_row, 1))
    flip = 2
    while flip < n_row:
        mine = sorted(d for d in acts if d % 2 == 0)
        got = lax.ppermute(jnp.stack([acts[d] for d in mine]), "row", _pairs(n_row, flip))
        for i, d in enumerate(mine):
            acts[d ^ flip] = got[i]
        flip *= 2

    def down_pair(d):
        lo, hi = acts[d], acts[d ^ 1]
        pair = jnp.where(core == 0, jnp.concatenate([lo, hi], axis=1),
                         jnp.concatenate([hi, lo], axis=1))
        w = lax.dynamic_slice_in_dim(down_weight, ((r ^ d) // 2) * 2 * quarter, 2 * quarter, 0)
        return jnp.dot(pair, w, precision=lax.Precision.HIGH,
                       preferred_element_type=jnp.float32)

    partial_out = down_pair(0)
    far = sorted(d for d in acts if d % 2 == 0 and d != 0)
    if far:
        stacked, partial_out = lax.optimization_barrier(
            (jnp.stack([acts[d] for d in far]), partial_out))
        got = lax.ppermute(stacked, "row", _pairs(n_row, 1))
        for i, d in enumerate(far):
            acts[d ^ 1] = got[i]
        for d in far:
            partial_out = partial_out + down_pair(d)
    per_chunk = partial_out.shape[0] // N_CHUNK
    out_share = jnp.concatenate(
        [_scatter_rel(partial_out[i * per_chunk:(i + 1) * per_chunk], "col", n_col)
         for i in range(N_CHUNK)], axis=0)
    back = _exchange_abs(out_share.reshape(n_row, tok_dev, d_blk), "row", n_row, r)
    returned = back.swapaxes(0, 1).reshape(tok_dev, n_row * d_blk)
    return tokens + gate_vec * (returned + down_bias)


def solution(mesh):
    in_specs = (
        P(("groups", "row", "col"), None),
        P(None, "groups", None),
        P("row", "col"),
        P("col"),
        P("col", "row"),
        P(),
    )
    out_specs = P(("groups", "row", "col"), None)
    return jax.shard_map(local, mesh=mesh, in_specs=in_specs, out_specs=out_specs, check_vma=False)
```

```python
import jax
import jax.numpy as jnp
from jax import lax
from jax.sharding import PartitionSpec as P
from jax.experimental import pallas as pl
from jax.experimental.pallas import tpu as pltpu

SEQ = 256
N_CHUNK = 2


layer_eps = 1e-06


def _pairs(n, flip):
    return [(i, i ^ flip) for i in range(n)]


def _gather_rel(x, axis, n):
    held = {0: x}
    flip = n // 2
    while flip >= 1:
        keys = sorted(held)
        got = lax.ppermute(jnp.stack([held[k] for k in keys]), axis, _pairs(n, flip))
        for i, k in enumerate(keys):
            held[k ^ flip] = got[i]
        flip //= 2
    return jnp.concatenate([held[d] for d in range(n)], axis=0)


def _scatter_rel(x, axis, n):
    blk = x.shape[0] // n
    held = {d: x[d * blk:(d + 1) * blk] for d in range(n)}
    flip = 1
    while flip < n:
        sent = [d for d in sorted(held) if d & flip]
        got = lax.ppermute(jnp.stack([held[d] for d in sent]), axis, _pairs(n, flip))
        held = {d ^ flip: held[d ^ flip] + got[i] for i, d in enumerate(sent)}
        flip *= 2
    return held[0]


def _exchange_abs(blocks, axis, n, idx):
    got = [blocks[idx]]
    for d in range(1, n):
        got.append(lax.ppermute(blocks[idx ^ d], axis, _pairs(n, d)))
    rel = jnp.stack(got)
    return jnp.stack([rel[s ^ idx] for s in range(n)])


def _norm_kernel(x_ref, o_ref):
    x = x_ref[...]
    average = jnp.mean(x, axis=1, keepdims=True)
    centred = x - average
    spread_sq = jnp.mean(centred * centred, axis=1, keepdims=True)
    o_ref[...] = centred * lax.rsqrt(spread_sq + layer_eps)


def _normalize(tokens):
    rows, width = tokens.shape
    return pl.pallas_call(
        _norm_kernel,
        out_shape=jax.ShapeDtypeStruct(tokens.shape, jnp.float32),
        in_specs=[pl.BlockSpec(memory_space=pltpu.VMEM)],
        out_specs=pl.BlockSpec(memory_space=pltpu.VMEM),
        cost_estimate=pl.CostEstimate(flops=6 * rows * width, transcendentals=rows,
                                      bytes_accessed=8 * rows * width),
    )(tokens)


def local(tokens, modulation, up_weight, up_bias, down_weight, down_bias):
    n_row = lax.axis_size("row")
    tok_dev = tokens.shape[0]
    first_tok = (lax.axis_index("row") * lax.axis_size("col") + lax.axis_index("col")) * tok_dev
    sample = first_tok // SEQ
    own_mods = lax.dynamic_slice_in_dim(modulation, sample, 1, 1)[:, 0]
    shift_vec = own_mods[0]
    scale_vec = own_mods[1]
    gate_vec = own_mods[2]
    normed = _normalize(tokens)
    mixed = normed * (1.0 + scale_vec) + shift_vec
    r = lax.axis_index("row")
    d_blk = mixed.shape[1] // n_row
    sent_in = mixed.reshape(tok_dev, n_row, d_blk).swapaxes(0, 1)
    columns = _exchange_abs(sent_in, "row", n_row, r).reshape(n_row * tok_dev, d_blk)
    n_col = lax.axis_size("col")
    chunk = columns.shape[0] // N_CHUNK
    gathered = jnp.concatenate(
        [_gather_rel(columns[i * chunk:(i + 1) * chunk], "col", n_col) for i in range(N_CHUNK)],
        axis=0)
    n_pos = gathered.shape[0]
    ff_blk = up_weight.shape[1]
    quarter = ff_blk // n_row

    def up_block(d, lhs):
        w = lax.dynamic_slice_in_dim(up_weight, (r ^ d) * quarter, quarter, 1)
        return jnp.dot(lhs, w, precision=lax.Precision.HIGH,
                       preferred_element_type=jnp.float32)

    def low_bit(d):
        return (d & -d) if d else 2 * n_row

    core = r % 2

    def up_pair(d, lhs):
        w = lax.dynamic_slice_in_dim(up_weight, ((r ^ d) // 2) * 2 * quarter, 2 * quarter, 1)
        both = lax.optimization_barrier(
            jnp.dot(lhs, w, precision=lax.Precision.HIGH,
                    preferred_element_type=jnp.float32))
        lo, hi = both[:, :quarter], both[:, quarter:]
        mine = jnp.where(core == 0, lo, hi)
        other = jnp.where(core == 0, hi, lo)
        return mine, other

    held = {}
    lhs = gathered
    for i, d_even in enumerate(sorted(range(0, n_row, 2), key=low_bit)):
        if d_even:
            mine, other = up_pair(d_even, lhs)
        else:
            other = lax.optimization_barrier(up_block(1, lhs))
            mine = lax.optimization_barrier(up_block(0, lhs))
        held[d_even] = mine + lax.ppermute(other, "row", _pairs(n_row, 1))
    flip = 2
    while flip < n_row:
        sent = [d for d in sorted(held) if d & flip]
        got = lax.ppermute(jnp.stack([held[d] for d in sent]), "row", _pairs(n_row, flip))
        held = {d ^ flip: held[d ^ flip] + got[i] for i, d in enumerate(sent)}
        flip *= 2
    bias_q = lax.dynamic_slice_in_dim(up_bias, r * quarter, quarter)
    acts = {0: jax.nn.gelu(held[0] + bias_q[None, :], approximate=True)}
    acts[1] = lax.ppermute(acts[0], "row", _pairs(n_row, 1))
    flip = 2
    while flip < n_row:
        mine = sorted(d for d in acts if d % 2 == 0)
        got = lax.ppermute(jnp.stack([acts[d] for d in mine]), "row", _pairs(n_row, flip))
        for i, d in enumerate(mine):
            acts[d ^ flip] = got[i]
        flip *= 2

    def down_pair(d):
        lo, hi = acts[d], acts[d ^ 1]
        pair = jnp.where(core == 0, jnp.concatenate([lo, hi], axis=1),
                         jnp.concatenate([hi, lo], axis=1))
        w = lax.dynamic_slice_in_dim(down_weight, ((r ^ d) // 2) * 2 * quarter, 2 * quarter, 0)
        return jnp.dot(pair, w, precision=lax.Precision.HIGH,
                       preferred_element_type=jnp.float32)

    partial_out = down_pair(0)
    far = sorted(d for d in acts if d % 2 == 0 and d != 0)
    if far:
        stacked, partial_out = lax.optimization_barrier(
            (jnp.stack([acts[d] for d in far]), partial_out))
        got = lax.ppermute(stacked, "row", _pairs(n_row, 1))
        for i, d in enumerate(far):
            acts[d ^ 1] = got[i]
        for d in far:
            partial_out = partial_out + down_pair(d)
    per_chunk = partial_out.shape[0] // N_CHUNK
    out_share = jnp.concatenate(
        [_scatter_rel(partial_out[i * per_chunk:(i + 1) * per_chunk], "col", n_col)
         for i in range(N_CHUNK)], axis=0)
    back = _exchange_abs(out_share.reshape(n_row, tok_dev, d_blk), "row", n_row, r)
    returned = back.swapaxes(0, 1).reshape(tok_dev, n_row * d_blk)
    return tokens + gate_vec * (returned + down_bias)


def solution(mesh):
    in_specs = (
        P(("groups", "row", "col"), None),
        P(None, "groups", None),
        P("row", "col"),
        P("col"),
        P("col", "row"),
        P(),
    )
    out_specs = P(("groups", "row", "col"), None)
    return jax.shard_map(local, mesh=mesh, in_specs=in_specs, out_specs=out_specs, check_vma=False)
```

```python
import jax
import jax.numpy as jnp
from jax import lax
from jax.sharding import PartitionSpec as P
from jax.experimental import pallas as pl
from jax.experimental.pallas import tpu as pltpu

SEQ = 256
N_CHUNK = 2


layer_eps = 1e-06


def _pairs(n, flip):
    return [(i, i ^ flip) for i in range(n)]


def _gather_rel(x, axis, n):
    held = {0: x}
    flip = n // 2
    while flip >= 1:
        keys = sorted(held)
        got = lax.ppermute(jnp.stack([held[k] for k in keys]), axis, _pairs(n, flip))
        for i, k in enumerate(keys):
            held[k ^ flip] = got[i]
        flip //= 2
    return jnp.concatenate([held[d] for d in range(n)], axis=0)


def _scatter_rel(x, axis, n):
    blk = x.shape[0] // n
    held = {d: x[d * blk:(d + 1) * blk] for d in range(n)}
    flip = 1
    while flip < n:
        sent = [d for d in sorted(held) if d & flip]
        got = lax.ppermute(jnp.stack([held[d] for d in sent]), axis, _pairs(n, flip))
        held = {d ^ flip: held[d ^ flip] + got[i] for i, d in enumerate(sent)}
        flip *= 2
    return held[0]


def _exchange_abs(blocks, axis, n, idx):
    got = [blocks[idx]]
    for d in range(1, n):
        got.append(lax.ppermute(blocks[idx ^ d], axis, _pairs(n, d)))
    rel = jnp.stack(got)
    return jnp.stack([rel[s ^ idx] for s in range(n)])


def _norm_kernel(x_ref, o_ref):
    x = x_ref[...]
    average = jnp.mean(x, axis=1, keepdims=True)
    centred = x - average
    spread_sq = jnp.mean(centred * centred, axis=1, keepdims=True)
    o_ref[...] = centred * lax.rsqrt(spread_sq + layer_eps)


def _normalize(tokens):
    rows, width = tokens.shape
    return pl.pallas_call(
        _norm_kernel,
        out_shape=jax.ShapeDtypeStruct(tokens.shape, jnp.float32),
        in_specs=[pl.BlockSpec(memory_space=pltpu.VMEM)],
        out_specs=pl.BlockSpec(memory_space=pltpu.VMEM),
        cost_estimate=pl.CostEstimate(flops=6 * rows * width, transcendentals=rows,
                                      bytes_accessed=8 * rows * width),
    )(tokens)


def local(tokens, modulation, up_weight, up_bias, down_weight, down_bias):
    n_row = lax.axis_size("row")
    tok_dev = tokens.shape[0]
    first_tok = (lax.axis_index("row") * lax.axis_size("col") + lax.axis_index("col")) * tok_dev
    sample = first_tok // SEQ
    own_mods = lax.dynamic_slice_in_dim(modulation, sample, 1, 1)[:, 0]
    shift_vec = own_mods[0]
    scale_vec = own_mods[1]
    gate_vec = own_mods[2]
    normed = _normalize(tokens)
    mixed = normed * (1.0 + scale_vec) + shift_vec
    r = lax.axis_index("row")
    d_blk = mixed.shape[1] // n_row
    sent_in = mixed.reshape(tok_dev, n_row, d_blk).swapaxes(0, 1)
    columns = _exchange_abs(sent_in, "row", n_row, r).reshape(n_row * tok_dev, d_blk)
    n_col = lax.axis_size("col")
    chunk = columns.shape[0] // N_CHUNK
    gathered = jnp.concatenate(
        [_gather_rel(columns[i * chunk:(i + 1) * chunk], "col", n_col) for i in range(N_CHUNK)],
        axis=0)
    n_pos = gathered.shape[0]
    ff_blk = up_weight.shape[1]
    quarter = ff_blk // n_row

    def up_block(d, lhs):
        w = lax.dynamic_slice_in_dim(up_weight, (r ^ d) * quarter, quarter, 1)
        return jnp.dot(lhs, w, precision=lax.Precision.HIGH,
                       preferred_element_type=jnp.float32)

    def low_bit(d):
        return (d & -d) if d else 2 * n_row

    core = r % 2

    def up_pair(d, lhs):
        w = lax.dynamic_slice_in_dim(up_weight, ((r ^ d) // 2) * 2 * quarter, 2 * quarter, 1)
        both = lax.optimization_barrier(
            jnp.dot(lhs, w, precision=lax.Precision.HIGH,
                    preferred_element_type=jnp.float32))
        lo, hi = both[:, :quarter], both[:, quarter:]
        mine = jnp.where(core == 0, lo, hi)
        other = jnp.where(core == 0, hi, lo)
        return mine, other

    held = {}
    lhs = gathered
    for i, d_even in enumerate(sorted(range(0, n_row, 2), key=low_bit)):
        if d_even:
            mine, other = up_pair(d_even, lhs)
        else:
            other = lax.optimization_barrier(up_block(1, lhs))
            mine = lax.optimization_barrier(up_block(0, lhs))
        held[d_even] = mine + lax.ppermute(other, "row", _pairs(n_row, 1))
        if not d_even:
            bias_q = lax.dynamic_slice_in_dim(up_bias, r * quarter, quarter)
            held[0] = lax.optimization_barrier(held[0] + bias_q[None, :])
    flip = 2
    while flip < n_row:
        sent = [d for d in sorted(held) if d & flip]
        got = lax.ppermute(jnp.stack([held[d] for d in sent]), "row", _pairs(n_row, flip))
        held = {d ^ flip: held[d ^ flip] + got[i] for i, d in enumerate(sent)}
        flip *= 2
    acts = {0: jax.nn.gelu(held[0], approximate=True)}
    acts[1] = lax.ppermute(acts[0], "row", _pairs(n_row, 1))
    flip = 2
    while flip < n_row:
        mine = sorted(d for d in acts if d % 2 == 0)
        got = lax.ppermute(jnp.stack([acts[d] for d in mine]), "row", _pairs(n_row, flip))
        for i, d in enumerate(mine):
            acts[d ^ flip] = got[i]
        flip *= 2

    def down_pair(d):
        lo, hi = acts[d], acts[d ^ 1]
        pair = jnp.where(core == 0, jnp.concatenate([lo, hi], axis=1),
                         jnp.concatenate([hi, lo], axis=1))
        w = lax.dynamic_slice_in_dim(down_weight, ((r ^ d) // 2) * 2 * quarter, 2 * quarter, 0)
        return jnp.dot(pair, w, precision=lax.Precision.HIGH,
                       preferred_element_type=jnp.float32)

    partial_out = down_pair(0)
    far = sorted(d for d in acts if d % 2 == 0 and d != 0)
    if far:
        stacked, partial_out = lax.optimization_barrier(
            (jnp.stack([acts[d] for d in far]), partial_out))
        got = lax.ppermute(stacked, "row", _pairs(n_row, 1))
        for i, d in enumerate(far):
            acts[d ^ 1] = got[i]
        for d in far:
            partial_out = partial_out + down_pair(d)
    per_chunk = partial_out.shape[0] // N_CHUNK
    out_share = jnp.concatenate(
        [_scatter_rel(partial_out[i * per_chunk:(i + 1) * per_chunk], "col", n_col)
         for i in range(N_CHUNK)], axis=0)
    back = _exchange_abs(out_share.reshape(n_row, tok_dev, d_blk), "row", n_row, r)
    returned = back.swapaxes(0, 1).reshape(tok_dev, n_row * d_blk)
    return tokens + gate_vec * (returned + down_bias)


def solution(mesh):
    in_specs = (
        P(("groups", "row", "col"), None),
        P(None, "groups", None),
        P("row", "col"),
        P("col"),
        P("col", "row"),
        P(),
    )
    out_specs = P(("groups", "row", "col"), None)
    return jax.shard_map(local, mesh=mesh, in_specs=in_specs, out_specs=out_specs, check_vma=False)
```

```python
import jax
import jax.numpy as jnp
from jax import lax
from jax.sharding import PartitionSpec as P
from jax.experimental import pallas as pl
from jax.experimental.pallas import tpu as pltpu

SEQ = 256
N_CHUNK = 2


layer_eps = 1e-06


def _pairs(n, flip):
    return [(i, i ^ flip) for i in range(n)]


def _gather_rel(x, axis, n):
    held = {0: x}
    flip = n // 2
    while flip >= 1:
        keys = sorted(held)
        got = lax.ppermute(jnp.stack([held[k] for k in keys]), axis, _pairs(n, flip))
        for i, k in enumerate(keys):
            held[k ^ flip] = got[i]
        flip //= 2
    return jnp.concatenate([held[d] for d in range(n)], axis=0)


def _scatter_rel(x, axis, n):
    blk = x.shape[0] // n
    held = {d: x[d * blk:(d + 1) * blk] for d in range(n)}
    flip = 1
    while flip < n:
        sent = [d for d in sorted(held) if d & flip]
        got = lax.ppermute(jnp.stack([held[d] for d in sent]), axis, _pairs(n, flip))
        held = {d ^ flip: held[d ^ flip] + got[i] for i, d in enumerate(sent)}
        flip *= 2
    return held[0]


def _exchange_abs(blocks, axis, n, idx):
    got = [blocks[idx]]
    for d in range(1, n):
        got.append(lax.ppermute(blocks[idx ^ d], axis, _pairs(n, d)))
    rel = jnp.stack(got)
    return jnp.stack([rel[s ^ idx] for s in range(n)])


def _norm_kernel(x_ref, o_ref):
    x = x_ref[...]
    average = jnp.mean(x, axis=1, keepdims=True)
    centred = x - average
    spread_sq = jnp.mean(centred * centred, axis=1, keepdims=True)
    o_ref[...] = centred * lax.rsqrt(spread_sq + layer_eps)


def _normalize(tokens):
    rows, width = tokens.shape
    return pl.pallas_call(
        _norm_kernel,
        out_shape=jax.ShapeDtypeStruct(tokens.shape, jnp.float32),
        in_specs=[pl.BlockSpec(memory_space=pltpu.VMEM)],
        out_specs=pl.BlockSpec(memory_space=pltpu.VMEM),
        cost_estimate=pl.CostEstimate(flops=6 * rows * width, transcendentals=rows,
                                      bytes_accessed=8 * rows * width),
    )(tokens)


def local(tokens, modulation, up_weight, up_bias, down_weight, down_bias):
    n_row = lax.axis_size("row")
    tok_dev = tokens.shape[0]
    first_tok = (lax.axis_index("row") * lax.axis_size("col") + lax.axis_index("col")) * tok_dev
    sample = first_tok // SEQ
    own_mods = lax.dynamic_slice_in_dim(modulation, sample, 1, 1)[:, 0]
    shift_vec = own_mods[0]
    scale_vec = own_mods[1]
    gate_vec = own_mods[2]
    normed = _normalize(tokens)
    mixed = normed * (1.0 + scale_vec) + shift_vec
    base = lax.optimization_barrier(tokens + gate_vec * down_bias)
    r = lax.axis_index("row")
    d_blk = mixed.shape[1] // n_row
    sent_in = mixed.reshape(tok_dev, n_row, d_blk).swapaxes(0, 1)
    columns = _exchange_abs(sent_in, "row", n_row, r).reshape(n_row * tok_dev, d_blk)
    n_col = lax.axis_size("col")
    chunk = columns.shape[0] // N_CHUNK
    gathered = jnp.concatenate(
        [_gather_rel(columns[i * chunk:(i + 1) * chunk], "col", n_col) for i in range(N_CHUNK)],
        axis=0)
    n_pos = gathered.shape[0]
    ff_blk = up_weight.shape[1]
    quarter = ff_blk // n_row

    def up_block(d, lhs):
        w = lax.dynamic_slice_in_dim(up_weight, (r ^ d) * quarter, quarter, 1)
        return jnp.dot(lhs, w, precision=lax.Precision.HIGH,
                       preferred_element_type=jnp.float32)

    def low_bit(d):
        return (d & -d) if d else 2 * n_row

    core = r % 2

    def up_pair(d, lhs):
        w = lax.dynamic_slice_in_dim(up_weight, ((r ^ d) // 2) * 2 * quarter, 2 * quarter, 1)
        both = lax.optimization_barrier(
            jnp.dot(lhs, w, precision=lax.Precision.HIGH,
                    preferred_element_type=jnp.float32))
        lo, hi = both[:, :quarter], both[:, quarter:]
        mine = jnp.where(core == 0, lo, hi)
        other = jnp.where(core == 0, hi, lo)
        return mine, other

    held = {}
    lhs = gathered
    for i, d_even in enumerate(sorted(range(0, n_row, 2), key=low_bit)):
        if d_even:
            mine, other = up_pair(d_even, lhs)
        else:
            other = lax.optimization_barrier(up_block(1, lhs))
            mine = lax.optimization_barrier(up_block(0, lhs))
        held[d_even] = mine + lax.ppermute(other, "row", _pairs(n_row, 1))
        if not d_even:
            bias_q = lax.dynamic_slice_in_dim(up_bias, r * quarter, quarter)
            held[0] = lax.optimization_barrier(held[0] + bias_q[None, :])
    flip = 2
    while flip < n_row:
        sent = [d for d in sorted(held) if d & flip]
        got = lax.ppermute(jnp.stack([held[d] for d in sent]), "row", _pairs(n_row, flip))
        held = {d ^ flip: held[d ^ flip] + got[i] for i, d in enumerate(sent)}
        flip *= 2
    acts = {0: jax.nn.gelu(held[0], approximate=True)}
    acts[1] = lax.ppermute(acts[0], "row", _pairs(n_row, 1))
    flip = 2
    while flip < n_row:
        mine = sorted(d for d in acts if d % 2 == 0)
        got = lax.ppermute(jnp.stack([acts[d] for d in mine]), "row", _pairs(n_row, flip))
        for i, d in enumerate(mine):
            acts[d ^ flip] = got[i]
        flip *= 2

    def down_pair(d):
        lo, hi = acts[d], acts[d ^ 1]
        pair = jnp.where(core == 0, jnp.concatenate([lo, hi], axis=1),
                         jnp.concatenate([hi, lo], axis=1))
        w = lax.dynamic_slice_in_dim(down_weight, ((r ^ d) // 2) * 2 * quarter, 2 * quarter, 0)
        return jnp.dot(pair, w, precision=lax.Precision.HIGH,
                       preferred_element_type=jnp.float32)

    partial_out = down_pair(0)
    far = sorted(d for d in acts if d % 2 == 0 and d != 0)
    if far:
        stacked, partial_out = lax.optimization_barrier(
            (jnp.stack([acts[d] for d in far]), partial_out))
        got = lax.ppermute(stacked, "row", _pairs(n_row, 1))
        for i, d in enumerate(far):
            acts[d ^ 1] = got[i]
        for d in far:
            partial_out = partial_out + down_pair(d)
    per_chunk = partial_out.shape[0] // N_CHUNK
    out_share = jnp.concatenate(
        [_scatter_rel(partial_out[i * per_chunk:(i + 1) * per_chunk], "col", n_col)
         for i in range(N_CHUNK)], axis=0)
    back = _exchange_abs(out_share.reshape(n_row, tok_dev, d_blk), "row", n_row, r)
    returned = back.swapaxes(0, 1).reshape(tok_dev, n_row * d_blk)
    return base + gate_vec * returned


def solution(mesh):
    in_specs = (
        P(("groups", "row", "col"), None),
        P(None, "groups", None),
        P("row", "col"),
        P("col"),
        P("col", "row"),
        P(),
    )
    out_specs = P(("groups", "row", "col"), None)
    return jax.shard_map(local, mesh=mesh, in_specs=in_specs, out_specs=out_specs, check_vma=False)
```
